32 devices in a mesh: row: 8 (over z, y), col: 4 (over x, core).
Axes of the slice: x: 2, y: 2, z: 4, core: 2. Of those that a mesh axis runs over, the one named last changes fastest.
Arguments:
- x_t: bfloat16 [128, 8192], P('col', 'row'), may hold values from -6 to 6
- tiles: bfloat16 [64, 128, 128], P('row'), may hold values from -0.375 to 0.375
- tile_owner: int32 [64, 1], P('row'), may hold values from 0 to 7; in each aligned block of 8 rows (0 to 7, 8 to 15, ...) at most 2 rows name the same one
- tile_local: int32 [64, 2], P('row'), may hold values from 0 to 7
- weight: bfloat16 [128, 256], replicated, may hold values from -0.5 to 0.5
- cotangent: bfloat16 [8192, 256], P('row'), may hold values from -0.0625 to 0.0625
Outputs:
- act: bfloat16 [8192, 256], P('row')
- grad_w: float32 [128, 256], P('col')
The draws below stay inside these ranges and needn't reach their ends.
Inputs may be any that keep to these rules, and one draw needn't show every extreme that they name: `tile_owner`: within the 8 stored tiles of one index of row (aligned blocks of 8 rows) no owner appears more than 2 times, and some owner appears exactly 2 times.
All inputs are finite; a program needn't handle non-finite values.
Results may differ from the reference program's by a relative error of at most 0.0059.
Values may be sent and summed in bfloat16 or wider, within the bound.
No kernel may reach another device: no remote copies, remote signals or barrier semaphores. Data moves between devices by JAX's collectives and lax.ppermute only.
A program may use at most 64 MiB of HBM per device.

```python
import math
import jax
import jax.numpy as jnp
import numpy as np
from jax import lax

FEAT = 128
HID = 256
TILE_DIM = 128
NB_DEV = 8
TILES = 8
TILES_ALL = 64
CAP = 2
NODES = 8192
N_ROW = 8


def place_ends(values, own_key, low, largest):
    place = [jax.random.randint(jax.random.fold_in(own_key, axis), (), 0, length) for axis, length in enumerate(values.shape)]
    main_axis = values.shape.index(max(values.shape))
    neighbour = place[:main_axis] + [(place[main_axis] + 1) % values.shape[main_axis]] + place[main_axis + 1:]
    return values.at[tuple(place)].set(low).at[tuple(neighbour)].set(largest)


def steps_of(own_key, extent, pieces, least, largest):
    def one(axis_at, parts):
        steps = jax.random.uniform(jax.random.fold_in(jax.random.fold_in(own_key, 6), axis_at), (parts,), jnp.float32, least / len(pieces), largest / len(pieces))
        return jnp.repeat(jnp.exp(steps), extent[axis_at] // parts).reshape((-1,) + (1,) * (len(extent) - axis_at - 1))

    loudness = one(*pieces[0])
    for cut in pieces[1:]:
        loudness = loudness * one(*cut)
    return loudness


def assign_block(stream_key, own, number, rows, amount, top, reach, skew):
    sequence = jax.random.permutation(stream_key, amount)
    packed, ordinary = shares(amount, rows * top, reach, skew, True), shares(amount, rows * top, reach, skew, False)
    places = jnp.arange(amount)

    def named(tallies, offset_by):
        used = int((tallies > 0).sum())
        fixed = max(1, used // 4)
        passed = fixed + (places - fixed + offset_by * (used - fixed)) % max(1, amount - fixed)
        return jnp.zeros((amount,), jnp.int32).at[sequence[jnp.where(places < fixed, places, passed)]].set(jnp.asarray(tallies, jnp.int32))

    tallies = jnp.where(number % 4 == 0, named(packed, number // 4), named(ordinary, number - number // 4 - 1))
    mixed = jax.random.permutation(jax.random.fold_in(own, 3), amount)
    source_of, sink = mixed[0:amount // 2 * 2:2], mixed[1:amount // 2 * 2:2]
    slack = jnp.minimum(tallies[source_of] - 1, reach - tallies[sink]) // 2
    slack = jnp.where((source_of == sequence[0]) | (sink == sequence[0]) | (tallies[sink] == 0), 0, jnp.maximum(slack, 0))
    passed = jax.random.randint(jax.random.fold_in(own, 4), (amount // 2,), 0, 1 << 20) % (slack + 1)
    tallies = tallies.at[source_of].add(-passed).at[sink].add(passed)
    items = jnp.searchsorted(jnp.cumsum(tallies), jnp.arange(rows * top), side="right").astype(jnp.int32)
    table = items.reshape(top, rows).T
    table = table[jax.random.permutation(jax.random.fold_in(own, 1), rows)]
    offset_by = jax.random.randint(jax.random.fold_in(own, 2), (rows, 1), 0, top)
    return jnp.take_along_axis(table, (jnp.arange(top)[None, :] + offset_by) % top, axis=1)


def shares(amount, total, most, slope, full):
    portions = [(1 << 20) // math.isqrt(grade ** slope) + 1 for grade in range(1, amount + 1)]
    largest = most if full else min(most, max(-(-total // amount), total * portions[0] // sum(portions)))
    least = 1 if total - largest >= amount - 1 else 0
    holding, surplus = [largest] + [least] * (amount - 1), total - largest - least * (amount - 1)
    while surplus > 0:
        candidates = [i for i in range(1, amount) if holding[i] < largest] or [i for i in range(1, amount) if holding[i] < most]
        pool, remaining = sum([portions[i] for i in candidates]), surplus
        for i in candidates:
            more = min(most - holding[i], max(1, remaining * portions[i] // pool), surplus)
            holding[i] = holding[i] + more
            surplus = surplus - more
    return np.array(holding)


def bell_draw(key, extent, deviation, reach, cuts=(), dtype=jnp.bfloat16):
    gain = steps_of(key, extent, cuts, -0.22, 0.18) if cuts else 1.0
    drawn = jax.random.normal(key, extent, jnp.float32) * deviation * gain
    return jnp.minimum(jnp.maximum(drawn, -reach), reach).astype(dtype)


def setup_inputs(seed: int = 0) -> dict:
    keys = jax.random.split(jax.random.key(seed), 7)
    x_t = bell_draw(keys[0], (FEAT, NODES), 1.0, 6.0, ((0, 4), (1, 8)))
    tiles = bell_draw(keys[1], (TILES_ALL, TILE_DIM, TILE_DIM), (2 * TILES * TILE_DIM // NB_DEV) ** -0.5, 0.375, ((0, 8),))
    tile_owner_keys = jax.random.split(jax.random.fold_in(keys[2], 1), TILES_ALL // TILES)
    tile_owner_turns = jax.random.permutation(jax.random.fold_in(keys[2], 3), TILES_ALL // TILES)
    tile_owner = jax.vmap(lambda own, number: assign_block(jax.random.fold_in(keys[2], 2), own, number, TILES, N_ROW, 1, CAP, 2))(tile_owner_keys, tile_owner_turns).reshape((TILES_ALL, 1))
    tile_local = place_ends(jax.random.randint(keys[3], (TILES_ALL, 2), 0, NB_DEV), jax.random.fold_in(keys[3], 1), 0, NB_DEV - 1).astype(jnp.int32)
    weight = bell_draw(keys[4], (FEAT, HID), FEAT ** -0.5, 0.5)
    cotangent = bell_draw(keys[5], (NODES, HID), NODES ** -0.5, 0.0625, ((0, 8),))
    return {"x_t": x_t, "tiles": tiles, "tile_owner": tile_owner, "tile_local": tile_local, "weight": weight, "cotangent": cotangent}


def reference(x_t, tiles, tile_owner, tile_local, weight, cotangent):
    nodes = x_t.shape[1]
    blocks = nodes // TILE_DIM
    xb = x_t.reshape(FEAT, blocks, TILE_DIM).transpose(1, 0, 2)

    def group(carry, index):
        start = (index * TILES).astype(jnp.int32)
        part = lax.dynamic_slice_in_dim(tiles, start, TILES, 0).astype(jnp.float32)
        owner = lax.dynamic_slice_in_dim(tile_owner, start, TILES, 0)[:, 0]
        local = lax.dynamic_slice_in_dim(tile_local, start, TILES, 0)
        row_blk = (index * NB_DEV).astype(jnp.int32) + local[:, 0]
        col_blk = owner * NB_DEV + local[:, 1]
        source = jnp.take(xb, col_blk, axis=0).astype(jnp.float32)
        own = jnp.take(xb, row_blk, axis=0).astype(jnp.float32)
        forward = jnp.einsum('tfj,tij->tfi', source, part)
        mirror = jnp.einsum('tfi,tij->tfj', own, part)
        mirror = lax.optimization_barrier(mirror.astype(jnp.bfloat16)).astype(jnp.float32)
        carry = carry.at[row_blk].add(forward).at[col_blk].add(mirror)
        return carry, None

    start_acc = jnp.zeros((blocks, FEAT, TILE_DIM), jnp.float32)
    accum, _ = lax.scan(group, start_acc, jnp.arange(N_ROW).astype(jnp.int32))
    z_t = accum.astype(jnp.bfloat16).transpose(1, 0, 2).reshape(FEAT, nodes)
    y = lax.dot_general(z_t, weight, (((0,), (0,)), ((), ())), preferred_element_type=jnp.float32)
    act = jax.nn.silu(y).astype(jnp.bfloat16)
    sig = jax.nn.sigmoid(y)
    grad_y = (cotangent.astype(jnp.float32) * sig * (1.0 + y * (1.0 - sig))).astype(jnp.bfloat16)
    grad_w = jnp.dot(z_t, grad_y, preferred_element_type=jnp.float32)
    return act, grad_w
```

```python
import jax
import jax.numpy as jnp
from jax import lax
from jax.sharding import PartitionSpec as P


def gather_groups(z_part, n_col):
    if n_col == 1:
        return z_part
    me = lax.axis_index("col")
    parts = [z_part]
    for k in range(1, n_col):
        perm = [(i, (i + k) % n_col) for i in range(n_col)]
        parts.append(lax.ppermute(z_part, "col", perm))
    stacked = jnp.stack(parts)
    order = (me - jnp.arange(n_col, dtype=jnp.int32)) % n_col
    full = jnp.take(stacked, order, axis=0)
    return full.reshape(n_col * z_part.shape[0], z_part.shape[1])


def sum_over_row(x, n_row):
    if n_row & (n_row - 1):
        return lax.psum(x, "row")
    k = 1
    while k < n_row:
        perm = [(i, i ^ k) for i in range(n_row)]
        x = x + lax.ppermute(x, "row", perm)
        k *= 2
    return x


def body(x_t, tiles, tile_owner, tile_local, weight, cotangent):
    n_row = lax.axis_size("row")
    n_col = lax.axis_size("col")
    n_tiles, tile_dim = (tiles.shape[0], tiles.shape[1])
    feat_q, rows = x_t.shape
    n_blocks = rows // tile_dim
    capacity = 2 * (n_tiles // n_row)
    xb = x_t.reshape(feat_q, n_blocks, tile_dim).transpose(1, 0, 2)
    flat_blocks = xb.reshape(n_blocks, feat_q * tile_dim)
    owner = tile_owner[:, 0]
    row_local = tile_local[:, 0]
    col_local = tile_local[:, 1]
    owner_hot = (owner[:, None] == jnp.arange(n_row, dtype=jnp.int32)[None, :]).astype(jnp.int32)
    rank = jnp.sum(owner_hot * (jnp.cumsum(owner_hot, axis=0) - 1), axis=1)
    slot = owner * capacity + rank
    requests = (
        jnp.zeros((n_row * capacity,), jnp.int32).at[slot].set(col_local).reshape(n_row, capacity)
    )
    own_blocks = jnp.take(xb, row_local, axis=0)
    mirror_terms = jnp.einsum(
        "tfi,tij->tfj", own_blocks, tiles, preferred_element_type=jnp.float32
    ).astype(jnp.bfloat16)
    outgoing = jnp.zeros((n_row * capacity, feat_q * tile_dim), jnp.bfloat16)
    outgoing = (
        outgoing.at[slot]
        .set(mirror_terms.reshape(n_tiles, feat_q * tile_dim))
        .reshape(n_row, capacity, feat_q * tile_dim)
    )
    block_ids = lax.all_to_all(requests, "row", split_axis=0, concat_axis=0, tiled=True)
    picked = jnp.take(flat_blocks, block_ids, axis=0)
    both = lax.all_to_all(
        jnp.concatenate([picked, outgoing], axis=1), "row", split_axis=0, concat_axis=0, tiled=True
    )
    fetched = both[:, :capacity]
    incoming = both[:, capacity:]
    fetched_tiles = jnp.take(fetched.reshape(n_row * capacity, feat_q, tile_dim), slot, axis=0)
    forward_terms = jnp.einsum(
        "tfj,tij->tfi", fetched_tiles, tiles, preferred_element_type=jnp.float32
    )
    block_range = jnp.arange(n_blocks, dtype=jnp.int32)
    row_hot = (row_local[:, None] == block_range[None, :]).astype(jnp.float32)
    local_sum = jnp.einsum("tfi,tb->fbi", forward_terms, row_hot, precision=lax.Precision.HIGHEST)
    in_hot = (block_ids.reshape(-1)[:, None] == block_range[None, :]).astype(jnp.bfloat16)
    mirror_sum = jnp.einsum(
        "sk,sb->bk",
        incoming.reshape(n_row * capacity, feat_q * tile_dim),
        in_hot,
        preferred_element_type=jnp.float32,
    )
    mirror_sum = mirror_sum.reshape(n_blocks, feat_q, tile_dim).transpose(1, 0, 2)
    z_part = (local_sum + mirror_sum).reshape(feat_q, rows).astype(jnp.bfloat16)
    z_full = gather_groups(z_part, n_col)
    y_full = lax.dot_general(
        z_full, weight, (((0,), (0,)), ((), ())), preferred_element_type=jnp.float32
    )
    act = jax.nn.silu(y_full).astype(jnp.bfloat16)
    sig = jax.nn.sigmoid(y_full)
    grad_y = (cotangent.astype(jnp.float32) * sig * (1.0 + y_full * (1.0 - sig))).astype(
        jnp.bfloat16
    )
    grad_part = jnp.dot(z_part, grad_y, preferred_element_type=jnp.float32)
    grad_w = sum_over_row(grad_part, n_row)
    return (act, grad_w)


def solution(mesh):
    in_specs = (
        P("col", "row"),
        P("row", None, None),
        P("row", None),
        P("row", None),
        P(),
        P("row", None),
    )
    out_specs = (P("row", None), P("col", None))
    return jax.shard_map(body, mesh=mesh, in_specs=in_specs, out_specs=out_specs, check_vma=False)
```

```python
import jax
import jax.numpy as jnp
from jax import lax
from jax.sharding import PartitionSpec as P


def gather_groups(z_part, n_col):
    if n_col == 1:
        return z_part
    me = lax.axis_index("col")
    parts = [z_part]
    for k in range(1, n_col):
        perm = [(i, (i + k) % n_col) for i in range(n_col)]
        parts.append(lax.ppermute(z_part, "col", perm))
    stacked = jnp.stack(parts)
    order = (me - jnp.arange(n_col, dtype=jnp.int32)) % n_col
    full = jnp.take(stacked, order, axis=0)
    return full.reshape(n_col * z_part.shape[0], z_part.shape[1])


def sum_over_row(x, n_row):
    if n_row & (n_row - 1):
        return lax.psum(x, "row")
    k = 1
    while k < n_row:
        perm = [(i, i ^ k) for i in range(n_row)]
        x = x + lax.ppermute(x, "row", perm)
        k *= 2
    return x


def body(x_t, tiles, tile_owner, tile_local, weight, cotangent):
    n_row = lax.axis_size("row")
    n_col = lax.axis_size("col")
    n_tiles, tile_dim = (tiles.shape[0], tiles.shape[1])
    feat_q, rows = x_t.shape
    n_blocks = rows // tile_dim
    capacity = 2 * (n_tiles // n_row)
    xb = x_t.reshape(feat_q, n_blocks, tile_dim).transpose(1, 0, 2)
    flat_blocks = xb.reshape(n_blocks, feat_q * tile_dim)
    owner = tile_owner[:, 0]
    row_local = tile_local[:, 0]
    col_local = tile_local[:, 1]
    owner_hot = (owner[:, None] == jnp.arange(n_row, dtype=jnp.int32)[None, :]).astype(jnp.int32)
    rank = jnp.sum(owner_hot * (jnp.cumsum(owner_hot, axis=0) - 1), axis=1)
    slot = owner * capacity + rank
    slot_ids = (
        jnp.zeros((n_row * capacity,), jnp.int32).at[slot].set(col_local).reshape(n_row, capacity)
    )
    id_rows = jnp.zeros((n_row, 1, feat_q * tile_dim), jnp.bfloat16)
    id_rows = id_rows.at[:, 0, :capacity].set(slot_ids.astype(jnp.bfloat16))
    own_blocks = jnp.take(xb, row_local, axis=0)
    mirror_terms = jnp.einsum(
        "tfi,tij->tfj", own_blocks, tiles, preferred_element_type=jnp.float32
    ).astype(jnp.bfloat16)
    outgoing = jnp.zeros((n_row * capacity, feat_q * tile_dim), jnp.bfloat16)
    outgoing = (
        outgoing.at[slot]
        .set(mirror_terms.reshape(n_tiles, feat_q * tile_dim))
        .reshape(n_row, capacity, feat_q * tile_dim)
    )
    every_block = jnp.broadcast_to(flat_blocks[None], (n_row, n_blocks, feat_q * tile_dim))
    payload = jnp.concatenate([every_block, outgoing, id_rows], axis=1)
    got = lax.all_to_all(payload, "row", split_axis=0, concat_axis=0, tiled=True)
    all_x = got[:, :n_blocks].reshape(n_row * n_blocks, feat_q, tile_dim)
    incoming = got[:, n_blocks : n_blocks + capacity]
    block_ids = got[:, n_blocks + capacity, :capacity].astype(jnp.int32)
    fetched_tiles = jnp.take(all_x, owner * n_blocks + col_local, axis=0)
    forward_terms = jnp.einsum(
        "tfj,tij->tfi", fetched_tiles, tiles, preferred_element_type=jnp.float32
    )
    block_range = jnp.arange(n_blocks, dtype=jnp.int32)
    row_hot = (row_local[:, None] == block_range[None, :]).astype(jnp.float32)
    local_sum = jnp.einsum("tfi,tb->fbi", forward_terms, row_hot, precision=lax.Precision.HIGHEST)
    in_hot = (block_ids.reshape(-1)[:, None] == block_range[None, :]).astype(jnp.bfloat16)
    mirror_sum = jnp.einsum(
        "sk,sb->bk",
        incoming.reshape(n_row * capacity, feat_q * tile_dim),
        in_hot,
        preferred_element_type=jnp.float32,
    )
    mirror_sum = mirror_sum.reshape(n_blocks, feat_q, tile_dim).transpose(1, 0, 2)
    z_part = (local_sum + mirror_sum).reshape(feat_q, rows).astype(jnp.bfloat16)
    z_full = gather_groups(z_part, n_col)
    y_full = lax.dot_general(
        z_full, weight, (((0,), (0,)), ((), ())), preferred_element_type=jnp.float32
    )
    act = jax.nn.silu(y_full).astype(jnp.bfloat16)
    sig = jax.nn.sigmoid(y_full)
    grad_y = (cotangent.astype(jnp.float32) * sig * (1.0 + y_full * (1.0 - sig))).astype(
        jnp.bfloat16
    )
    grad_part = jnp.dot(z_part, grad_y, preferred_element_type=jnp.float32)
    grad_w = sum_over_row(grad_part, n_row)
    return (act, grad_w)


def solution(mesh):
    in_specs = (
        P("col", "row"),
        P("row", None, None),
        P("row", None),
        P("row", None),
        P(),
        P("row", None),
    )
    out_specs = (P("row", None), P("col", None))
    return jax.shard_map(body, mesh=mesh, in_specs=in_specs, out_specs=out_specs, check_vma=False)
```

```python
import jax
import jax.numpy as jnp
from jax import lax
from jax.sharding import PartitionSpec as P


def gather_groups(z_part, n_col):
    if n_col == 1:
        return z_part
    me = lax.axis_index("col")
    parts = [z_part]
    for k in range(1, n_col):
        perm = [(i, (i + k) % n_col) for i in range(n_col)]
        parts.append(lax.ppermute(z_part, "col", perm))
    stacked = jnp.stack(parts)
    order = (me - jnp.arange(n_col, dtype=jnp.int32)) % n_col
    full = jnp.take(stacked, order, axis=0)
    return full.reshape(n_col * z_part.shape[0], z_part.shape[1])


def sum_over_row(x, n_row):
    every = jnp.broadcast_to(x[None], (n_row,) + x.shape)
    parts = lax.all_to_all(every, "row", split_axis=0, concat_axis=0, tiled=True)
    total = parts[0]
    for i in range(1, n_row):
        total = total + parts[i]
    return total


def body(x_t, tiles, tile_owner, tile_local, weight, cotangent):
    n_row = lax.axis_size("row")
    n_col = lax.axis_size("col")
    n_tiles, tile_dim = (tiles.shape[0], tiles.shape[1])
    feat_q, rows = x_t.shape
    n_blocks = rows // tile_dim
    capacity = 2 * (n_tiles // n_row)
    xb = x_t.reshape(feat_q, n_blocks, tile_dim).transpose(1, 0, 2)
    flat_blocks = xb.reshape(n_blocks, feat_q * tile_dim)
    owner = tile_owner[:, 0]
    row_local = tile_local[:, 0]
    col_local = tile_local[:, 1]
    owner_hot = (owner[:, None] == jnp.arange(n_row, dtype=jnp.int32)[None, :]).astype(jnp.int32)
    rank = jnp.sum(owner_hot * (jnp.cumsum(owner_hot, axis=0) - 1), axis=1)
    slot = owner * capacity + rank
    requests = (
        jnp.zeros((n_row * capacity,), jnp.int32).at[slot].set(col_local).reshape(n_row, capacity)
    )
    own_blocks = jnp.take(xb, row_local, axis=0)
    mirror_terms = jnp.einsum(
        "tfi,tij->tfj", own_blocks, tiles, preferred_element_type=jnp.float32
    ).astype(jnp.bfloat16)
    outgoing = jnp.zeros((n_row * capacity, feat_q * tile_dim), jnp.bfloat16)
    outgoing = (
        outgoing.at[slot]
        .set(mirror_terms.reshape(n_tiles, feat_q * tile_dim))
        .reshape(n_row, capacity, feat_q * tile_dim)
    )
    block_ids = lax.all_to_all(requests, "row", split_axis=0, concat_axis=0, tiled=True)
    picked = jnp.take(flat_blocks, block_ids, axis=0)
    both = lax.all_to_all(
        jnp.concatenate([picked, outgoing], axis=1), "row", split_axis=0, concat_axis=0, tiled=True
    )
    fetched = both[:, :capacity]
    incoming = both[:, capacity:]
    fetched_tiles = jnp.take(fetched.reshape(n_row * capacity, feat_q, tile_dim), slot, axis=0)
    forward_terms = jnp.einsum(
        "tfj,tij->tfi", fetched_tiles, tiles, preferred_element_type=jnp.float32
    )
    block_range = jnp.arange(n_blocks, dtype=jnp.int32)
    row_hot = (row_local[:, None] == block_range[None, :]).astype(jnp.float32)
    local_sum = jnp.einsum("tfi,tb->fbi", forward_terms, row_hot, precision=lax.Precision.HIGHEST)
    in_hot = (block_ids.reshape(-1)[:, None] == block_range[None, :]).astype(jnp.bfloat16)
    mirror_sum = jnp.einsum(
        "sk,sb->bk",
        incoming.reshape(n_row * capacity, feat_q * tile_dim),
        in_hot,
        preferred_element_type=jnp.float32,
    )
    mirror_sum = mirror_sum.reshape(n_blocks, feat_q, tile_dim).transpose(1, 0, 2)
    z_part = (local_sum + mirror_sum).reshape(feat_q, rows).astype(jnp.bfloat16)
    z_full = gather_groups(z_part, n_col)
    y_full = lax.dot_general(
        z_full, weight, (((0,), (0,)), ((), ())), preferred_element_type=jnp.float32
    )
    act = jax.nn.silu(y_full).astype(jnp.bfloat16)
    sig = jax.nn.sigmoid(y_full)
    grad_y = (cotangent.astype(jnp.float32) * sig * (1.0 + y_full * (1.0 - sig))).astype(
        jnp.bfloat16
    )
    grad_part = jnp.dot(z_part, grad_y, preferred_element_type=jnp.float32)
    grad_w = sum_over_row(grad_part, n_row)
    return (act, grad_w)


def solution(mesh):
    in_specs = (
        P("col", "row"),
        P("row", None, None),
        P("row", None),
        P("row", None),
        P(),
        P("row", None),
    )
    out_specs = (P("row", None), P("col", None))
    return jax.shard_map(body, mesh=mesh, in_specs=in_specs, out_specs=out_specs, check_vma=False)
```

```python
import jax
import jax.numpy as jnp
from jax import lax
from jax.sharding import PartitionSpec as P


def rows_of(a, idx):
    return a.at[idx].get(mode="promise_in_bounds")


def gather_groups(z_part, n_col):
    if n_col == 1:
        return z_part
    me = lax.axis_index("col")
    parts = [z_part]
    for k in range(1, n_col):
        perm = [(i, (i + k) % n_col) for i in range(n_col)]
        parts.append(lax.ppermute(z_part, "col", perm))
    stacked = jnp.stack(parts)
    order = (me - jnp.arange(n_col, dtype=jnp.int32)) % n_col
    full = rows_of(stacked, order)
    return full.reshape(n_col * z_part.shape[0], z_part.shape[1])


def sum_over_row(x, n_row):
    every = jnp.broadcast_to(x[None], (n_row,) + x.shape)
    parts = lax.all_to_all(every, "row", split_axis=0, concat_axis=0, tiled=True)
    total = parts[0]
    for i in range(1, n_row):
        total = total + parts[i]
    return total


def body(x_t, tiles, tile_owner, tile_local, weight, cotangent):
    n_row = lax.axis_size("row")
    n_col = lax.axis_size("col")
    n_tiles, tile_dim = (tiles.shape[0], tiles.shape[1])
    feat_q, rows = x_t.shape
    n_blocks = rows // tile_dim
    capacity = 2 * (n_tiles // n_row)
    xb = x_t.reshape(feat_q, n_blocks, tile_dim).transpose(1, 0, 2)
    flat_blocks = xb.reshape(n_blocks, feat_q * tile_dim)
    owner = tile_owner[:, 0]
    row_local = tile_local[:, 0]
    col_local = tile_local[:, 1]
    tile_ids = jnp.arange(n_tiles, dtype=jnp.int32)
    same = owner[:, None] == owner[None, :]
    rank = jnp.sum((same & (tile_ids[None, :] < tile_ids[:, None])).astype(jnp.int32), axis=1)
    slot = owner * capacity + rank
    slot_range = jnp.arange(n_row * capacity, dtype=jnp.int32)
    slot_hot = slot[None, :] == slot_range[:, None]
    requests = jnp.sum(jnp.where(slot_hot, col_local[None, :], 0), axis=1)
    requests = jnp.broadcast_to(requests.reshape(n_row, capacity, 1), (n_row, capacity, 128))
    own_blocks = rows_of(xb, row_local)
    mirror_terms = jnp.einsum(
        "tfi,tij->tfj", own_blocks, tiles, preferred_element_type=jnp.float32
    ).astype(jnp.bfloat16)
    outgoing = jnp.zeros((n_row * capacity, feat_q * tile_dim), jnp.bfloat16)
    outgoing = outgoing.at[slot].set(
        mirror_terms.reshape(n_tiles, feat_q * tile_dim), mode="promise_in_bounds", unique_indices=True
    )
    source = jnp.concatenate([flat_blocks, outgoing], axis=0)
    got_ids = lax.all_to_all(requests, "row", split_axis=0, concat_axis=0, tiled=True)
    block_ids = got_ids[:, :, 0]
    mirror_rows = n_blocks + slot_range.reshape(n_row, capacity)
    pick = jnp.concatenate([block_ids, mirror_rows], axis=1)
    payload = rows_of(source, pick.reshape(-1)).reshape(n_row, 2 * capacity, feat_q * tile_dim)
    both = lax.all_to_all(payload, "row", split_axis=0, concat_axis=0, tiled=True)
    fetched = both[:, :capacity]
    incoming = both[:, capacity:]
    fetched_tiles = rows_of(fetched.reshape(n_row * capacity, feat_q, tile_dim), slot)
    forward_terms = jnp.einsum(
        "tfj,tij->tfi", fetched_tiles, tiles, preferred_element_type=jnp.float32
    )
    block_range = jnp.arange(n_blocks, dtype=jnp.int32)
    row_hot = (row_local[:, None] == block_range[None, :]).astype(jnp.float32)
    local_sum = jnp.einsum("tfi,tb->fbi", forward_terms, row_hot, precision=lax.Precision.HIGHEST)
    in_hot = (block_ids.reshape(-1)[:, None] == block_range[None, :]).astype(jnp.bfloat16)
    mirror_sum = jnp.einsum(
        "sk,sb->bk",
        incoming.reshape(n_row * capacity, feat_q * tile_dim),
        in_hot,
        preferred_element_type=jnp.float32,
    )
    mirror_sum = mirror_sum.reshape(n_blocks, feat_q, tile_dim).transpose(1, 0, 2)
    z_part = (local_sum + mirror_sum).reshape(feat_q, rows).astype(jnp.bfloat16)
    z_full = gather_groups(z_part, n_col)
    y_full = lax.dot_general(
        z_full, weight, (((0,), (0,)), ((), ())), preferred_element_type=jnp.float32
    )
    act = jax.nn.silu(y_full).astype(jnp.bfloat16)
    sig = jax.nn.sigmoid(y_full)
    grad_y = (cotangent.astype(jnp.float32) * sig * (1.0 + y_full * (1.0 - sig))).astype(
        jnp.bfloat16
    )
    grad_part = jnp.dot(z_part, grad_y, preferred_element_type=jnp.float32)
    grad_w = sum_over_row(grad_part, n_row)
    return (act, grad_w)


def solution(mesh):
    in_specs = (
        P("col", "row"),
        P("row", None, None),
        P("row", None),
        P("row", None),
        P(),
        P("row", None),
    )
    out_specs = (P("row", None), P("col", None))
    return jax.shard_map(body, mesh=mesh, in_specs=in_specs, out_specs=out_specs, check_vma=False)
```

```python
import jax
import jax.numpy as jnp
from jax import lax
from jax.sharding import PartitionSpec as P


def rows_of(a, idx):
    return a.at[idx].get(mode="promise_in_bounds")


def gather_groups(z_part, n_col):
    if n_col == 1:
        return z_part
    me = lax.axis_index("col")
    if n_col & (n_col - 1):
        parts = [z_part]
        for k in range(1, n_col):
            perm = [(i, (i + k) % n_col) for i in range(n_col)]
            parts.append(lax.ppermute(z_part, "col", perm))
        order = (me - jnp.arange(n_col, dtype=jnp.int32)) % n_col
        full = rows_of(jnp.stack(parts), order)
        return full.reshape(n_col * z_part.shape[0], z_part.shape[1])
    parts = [z_part]
    for k in range(1, n_col):
        parts.append(lax.ppermute(z_part, "col", [(i, i ^ k) for i in range(n_col)]))
    groups = []
    for j in range(n_col):
        pick = parts[n_col - 1]
        for k in range(n_col - 2, -1, -1):
            pick = jnp.where((me ^ k) == j, parts[k], pick)
        groups.append(pick)
    return jnp.concatenate(groups, axis=0)


def sum_over_row(x, n_row):
    every = jnp.broadcast_to(x[None], (n_row,) + x.shape)
    parts = lax.all_to_all(every, "row", split_axis=0, concat_axis=0, tiled=True)
    total = parts[0]
    for i in range(1, n_row):
        total = total + parts[i]
    return total


def body(x_t, tiles, tile_owner, tile_local, weight, cotangent):
    n_row = lax.axis_size("row")
    n_col = lax.axis_size("col")
    n_tiles, tile_dim = (tiles.shape[0], tiles.shape[1])
    feat_q, rows = x_t.shape
    n_blocks = rows // tile_dim
    capacity = 2 * (n_tiles // n_row)
    xb = x_t.reshape(feat_q, n_blocks, tile_dim).transpose(1, 0, 2)
    flat_blocks = xb.reshape(n_blocks, feat_q * tile_dim)
    owner = tile_owner[:, 0]
    row_local = tile_local[:, 0]
    col_local = tile_local[:, 1]
    tile_ids = jnp.arange(n_tiles, dtype=jnp.int32)
    same = owner[:, None] == owner[None, :]
    rank = jnp.sum((same & (tile_ids[None, :] < tile_ids[:, None])).astype(jnp.int32), axis=1)
    slot = owner * capacity + rank
    slot_range = jnp.arange(n_row * capacity, dtype=jnp.int32)
    slot_hot = slot[None, :] == slot_range[:, None]
    lane_slots = jnp.broadcast_to(slot_range.reshape(n_row, capacity, 1), (n_row, capacity, 128))
    requests = jnp.sum(
        jnp.where(slot[None, None, None, :] == lane_slots[..., None], col_local[None, None, None, :], 0),
        axis=-1,
    )
    own_blocks = rows_of(xb, row_local)
    mirror_terms = jnp.einsum(
        "tfi,tij->tfj", own_blocks, tiles, preferred_element_type=jnp.float32
    ).astype(jnp.bfloat16)
    outgoing = jnp.zeros((n_row * capacity, feat_q, tile_dim), jnp.bfloat16)
    outgoing = outgoing.at[slot].set(mirror_terms, mode="promise_in_bounds", unique_indices=True)
    source = jnp.concatenate([xb, outgoing], axis=0)
    got_ids = lax.all_to_all(requests, "row", split_axis=0, concat_axis=0, tiled=True)
    block_ids = got_ids[:, :, 0]
    mirror_rows = n_blocks + slot_range.reshape(n_row, capacity)
    pick = jnp.concatenate([block_ids, mirror_rows], axis=1)
    payload = rows_of(source, pick.reshape(-1)).reshape(n_row, 2 * capacity, feat_q, tile_dim)
    both = lax.all_to_all(payload, "row", split_axis=0, concat_axis=0, tiled=True)
    fetched = both[:, :capacity].reshape(n_row * capacity, feat_q, tile_dim)
    incoming = both[:, capacity:]
    fetched_tiles = rows_of(fetched, slot)
    forward_terms = jnp.einsum(
        "tfj,tij->tfi", fetched_tiles, tiles, preferred_element_type=jnp.float32
    )
    block_range = jnp.arange(n_blocks, dtype=jnp.int32)
    row_hot = (row_local[:, None] == block_range[None, :]).astype(jnp.float32)
    local_sum = jnp.einsum("tfi,tb->fbi", forward_terms, row_hot, precision=lax.Precision.HIGHEST)
    in_hot = (block_ids.reshape(-1)[:, None] == block_range[None, :]).astype(jnp.bfloat16)
    mirror_sum = jnp.einsum(
        "sk,sb->bk",
        incoming.reshape(n_row * capacity, feat_q * tile_dim),
        in_hot,
        preferred_element_type=jnp.float32,
    )
    mirror_sum = mirror_sum.reshape(n_blocks, feat_q, tile_dim).transpose(1, 0, 2)
    z_part = (local_sum + mirror_sum).reshape(feat_q, rows).astype(jnp.bfloat16)
    z_full = gather_groups(z_part, n_col)
    y_full = lax.dot_general(
        z_full, weight, (((0,), (0,)), ((), ())), preferred_element_type=jnp.float32
    )
    act = jax.nn.silu(y_full).astype(jnp.bfloat16)
    sig = jax.nn.sigmoid(y_full)
    grad_y = (cotangent.astype(jnp.float32) * sig * (1.0 + y_full * (1.0 - sig))).astype(
        jnp.bfloat16
    )
    grad_part = jnp.dot(z_part, grad_y, preferred_element_type=jnp.float32)
    grad_w = sum_over_row(grad_part, n_row)
    return (act, grad_w)


def solution(mesh):
    in_specs = (
        P("col", "row"),
        P("row", None, None),
        P("row", None),
        P("row", None),
        P(),
        P("row", None),
    )
    out_specs = (P("row", None), P("col", None))
    return jax.shard_map(body, mesh=mesh, in_specs=in_specs, out_specs=out_specs, check_vma=False)
```

```python
import jax
import jax.numpy as jnp
from jax import lax
from jax.sharding import PartitionSpec as P


def rows_of(a, idx):
    return a.at[idx].get(mode="promise_in_bounds")


def gather_groups(z_part, n_col):
    if n_col == 1:
        return z_part
    me = lax.axis_index("col")
    if n_col & (n_col - 1):
        parts = [z_part]
        for k in range(1, n_col):
            perm = [(i, (i + k) % n_col) for i in range(n_col)]
            parts.append(lax.ppermute(z_part, "col", perm))
        order = (me - jnp.arange(n_col, dtype=jnp.int32)) % n_col
        full = rows_of(jnp.stack(parts), order)
        return full.reshape(n_col * z_part.shape[0], z_part.shape[1])
    parts = [z_part]
    for k in range(1, n_col):
        parts.append(lax.ppermute(z_part, "col", [(i, i ^ k) for i in range(n_col)]))
    groups = []
    for j in range(n_col):
        pick = parts[n_col - 1]
        for k in range(n_col - 2, -1, -1):
            pick = jnp.where((me ^ k) == j, parts[k], pick)
        groups.append(pick)
    return jnp.concatenate(groups, axis=0)


def sum_over_row(x, n_row):
    every = jnp.broadcast_to(x[None], (n_row,) + x.shape)
    parts = lax.all_to_all(every, "row", split_axis=0, concat_axis=0, tiled=True)
    total = parts[0]
    for i in range(1, n_row):
        total = total + parts[i]
    return total


def body(x_t, tiles, tile_owner, tile_local, weight, cotangent):
    n_row = lax.axis_size("row")
    n_col = lax.axis_size("col")
    n_tiles, tile_dim = (tiles.shape[0], tiles.shape[1])
    feat_q, rows = x_t.shape
    n_blocks = rows // tile_dim
    capacity = 2 * (n_tiles // n_row)
    xb = x_t.reshape(feat_q, n_blocks, tile_dim).transpose(1, 0, 2)
    flat_blocks = xb.reshape(n_blocks, feat_q * tile_dim)
    owner = tile_owner[:, 0]
    row_local = tile_local[:, 0]
    col_local = tile_local[:, 1]
    tile_ids = jnp.arange(n_tiles, dtype=jnp.int32)
    same = owner[:, None] == owner[None, :]
    rank = jnp.sum((same & (tile_ids[None, :] < tile_ids[:, None])).astype(jnp.int32), axis=1)
    slot = owner * capacity + rank
    slot_range = jnp.arange(n_row * capacity, dtype=jnp.int32)
    slot_hot = slot[None, :] == slot_range[:, None]
    lane_slots = jnp.broadcast_to(slot_range.reshape(n_row, capacity, 1), (n_row, capacity, 128))
    requests = jnp.sum(
        jnp.where(slot[None, None, None, :] == lane_slots[..., None], col_local[None, None, None, :], 0),
        axis=-1,
    )
    own_blocks = rows_of(xb, row_local)
    mirror_terms = jnp.einsum(
        "tfi,tij->tfj", own_blocks, tiles, preferred_element_type=jnp.float32
    ).astype(jnp.bfloat16)
    outgoing = jnp.zeros((n_row * capacity, feat_q, tile_dim), jnp.bfloat16)
    outgoing = outgoing.at[slot].set(mirror_terms, mode="promise_in_bounds", unique_indices=True)
    source = jnp.concatenate([xb, outgoing], axis=0)
    got_ids = lax.all_to_all(requests, "row", split_axis=0, concat_axis=0, tiled=True)
    block_ids = got_ids[:, :, 0]
    mirror_rows = n_blocks + slot_range.reshape(n_row, capacity)
    pick = jnp.concatenate([block_ids, mirror_rows], axis=1)
    payload = rows_of(source, pick.reshape(-1)).reshape(n_row, 2 * capacity, feat_q, tile_dim)
    both = lax.all_to_all(payload, "row", split_axis=0, concat_axis=0, tiled=True)
    fetched = both[:, :capacity].reshape(n_row * capacity, feat_q, tile_dim)
    incoming = both[:, capacity:]
    fetched_tiles = rows_of(fetched, slot)
    forward_terms = jnp.einsum(
        "tfj,tij->tfi", fetched_tiles, tiles, preferred_element_type=jnp.float32
    )
    block_range = jnp.arange(n_blocks, dtype=jnp.int32)
    row_hot = (row_local[:, None] == block_range[None, :]).astype(jnp.float32)
    local_sum = jnp.einsum("tfi,tb->fbi", forward_terms, row_hot, precision=lax.Precision.HIGHEST)
    in_hot = (block_ids.reshape(-1)[:, None] == block_range[None, :]).astype(jnp.bfloat16)
    mirror_sum = jnp.einsum(
        "sk,sb->bk",
        incoming.reshape(n_row * capacity, feat_q * tile_dim),
        in_hot,
        preferred_element_type=jnp.float32,
    )
    mirror_sum = mirror_sum.reshape(n_blocks, feat_q, tile_dim).transpose(1, 0, 2)
    z_part = (local_sum + mirror_sum).reshape(feat_q, rows).astype(jnp.bfloat16)
    z_full = gather_groups(z_part, n_col)
    y_full = lax.dot_general(
        z_full, weight, (((0,), (0,)), ((), ())), preferred_element_type=jnp.float32
    )
    sig = jax.nn.sigmoid(y_full)
    grad_y = (cotangent.astype(jnp.float32) * sig * (1.0 + y_full * (1.0 - sig))).astype(
        jnp.bfloat16
    )
    grad_part = jnp.dot(z_part, grad_y, preferred_element_type=jnp.float32)
    y_late, grad_part = lax.optimization_barrier((y_full, grad_part))
    grad_w = sum_over_row(grad_part, n_row)
    act = jax.nn.silu(y_late).astype(jnp.bfloat16)
    return (act, grad_w)


def solution(mesh):
    in_specs = (
        P("col", "row"),
        P("row", None, None),
        P("row", None),
        P("row", None),
        P(),
        P("row", None),
    )
    out_specs = (P("row", None), P("col", None))
    return jax.shard_map(body, mesh=mesh, in_specs=in_specs, out_specs=out_specs, check_vma=False)
```

```python
import jax
import jax.numpy as jnp
from jax import lax
from jax.experimental import pallas as pl
from jax.experimental.pallas import tpu as pltpu
from jax.sharding import PartitionSpec as P


def rows_of(a, idx):
    return a.at[idx].get(mode="promise_in_bounds")


def gather_groups(z_part, n_col):
    if n_col == 1:
        return z_part
    me = lax.axis_index("col")
    if n_col & (n_col - 1):
        parts = [z_part]
        for k in range(1, n_col):
            perm = [(i, (i + k) % n_col) for i in range(n_col)]
            parts.append(lax.ppermute(z_part, "col", perm))
        order = (me - jnp.arange(n_col, dtype=jnp.int32)) % n_col
        full = rows_of(jnp.stack(parts), order)
        return full.reshape(n_col * z_part.shape[0], z_part.shape[1])
    parts = [z_part]
    for k in range(1, n_col):
        parts.append(lax.ppermute(z_part, "col", [(i, i ^ k) for i in range(n_col)]))
    groups = []
    for j in range(n_col):
        pick = parts[n_col - 1]
        for k in range(n_col - 2, -1, -1):
            pick = jnp.where((me ^ k) == j, parts[k], pick)
        groups.append(pick)
    return jnp.concatenate(groups, axis=0)


def sum_over_row(x, n_row):
    every = jnp.broadcast_to(x[None], (n_row,) + x.shape)
    parts = lax.all_to_all(every, "row", split_axis=0, concat_axis=0, tiled=True)
    total = parts[0]
    for i in range(1, n_row):
        total = total + parts[i]
    return total


def payload_kernel(ids_ref, slot_ref, xb_ref, mirror_ref, out_ref):
    n_row, two_cap = out_ref.shape[0], out_ref.shape[1]
    capacity = two_cap // 2
    zero = jnp.zeros(out_ref.shape[2:], out_ref.dtype)

    def fill(o, carry):
        for k in range(capacity):
            out_ref[o, k] = xb_ref[ids_ref[o, k, 0]]
            out_ref[o, capacity + k] = zero
        return carry

    lax.fori_loop(0, n_row, fill, 0)
    for t in range(mirror_ref.shape[0]):
        s = slot_ref[t]
        out_ref[s // capacity, capacity + s % capacity] = mirror_ref[t]


def build_payload(ids, slot, xb, mirror_terms, n_row, capacity):
    shape = (n_row, 2 * capacity) + xb.shape[1:]
    nbytes = 2 * (n_row * 2 * capacity + xb.shape[0] + mirror_terms.shape[0]) * xb.shape[1] * xb.shape[2]
    return pl.pallas_call(
        payload_kernel,
        out_shape=jax.ShapeDtypeStruct(shape, xb.dtype),
        in_specs=[
            pl.BlockSpec(memory_space=pltpu.SMEM),
            pl.BlockSpec(memory_space=pltpu.SMEM),
            pl.BlockSpec(memory_space=pltpu.VMEM),
            pl.BlockSpec(memory_space=pltpu.VMEM),
        ],
        out_specs=pl.BlockSpec(memory_space=pltpu.VMEM),
        cost_estimate=pl.CostEstimate(flops=0, transcendentals=0, bytes_accessed=nbytes),
    )(ids, slot, xb, mirror_terms)


def body(x_t, tiles, tile_owner, tile_local, weight, cotangent):
    n_row = lax.axis_size("row")
    n_col = lax.axis_size("col")
    n_tiles, tile_dim = (tiles.shape[0], tiles.shape[1])
    feat_q, rows = x_t.shape
    n_blocks = rows // tile_dim
    capacity = 2 * (n_tiles // n_row)
    xb = x_t.reshape(feat_q, n_blocks, tile_dim).transpose(1, 0, 2)
    flat_blocks = xb.reshape(n_blocks, feat_q * tile_dim)
    owner = tile_owner[:, 0]
    row_local = tile_local[:, 0]
    col_local = tile_local[:, 1]
    tile_ids = jnp.arange(n_tiles, dtype=jnp.int32)
    same = owner[:, None] == owner[None, :]
    rank = jnp.sum((same & (tile_ids[None, :] < tile_ids[:, None])).astype(jnp.int32), axis=1)
    slot = owner * capacity + rank
    slot_range = jnp.arange(n_row * capacity, dtype=jnp.int32)
    slot_hot = slot[None, :] == slot_range[:, None]
    lane_slots = jnp.broadcast_to(slot_range.reshape(n_row, capacity, 1), (n_row, capacity, 128))
    requests = jnp.sum(
        jnp.where(slot[None, None, None, :] == lane_slots[..., None], col_local[None, None, None, :], 0),
        axis=-1,
    )
    own_blocks = rows_of(xb, row_local)
    mirror_terms = jnp.einsum(
        "tfi,tij->tfj", own_blocks, tiles, preferred_element_type=jnp.float32
    ).astype(jnp.bfloat16)
    got_ids = lax.all_to_all(requests, "row", split_axis=0, concat_axis=0, tiled=True)
    block_ids = got_ids[:, :, 0]
    payload = build_payload(got_ids, slot, xb, mirror_terms, n_row, capacity)
    both = lax.all_to_all(payload, "row", split_axis=0, concat_axis=0, tiled=True)
    fetched = both[:, :capacity].reshape(n_row * capacity, feat_q, tile_dim)
    incoming = both[:, capacity:]
    fetched_tiles = rows_of(fetched, slot)
    forward_terms = jnp.einsum(
        "tfj,tij->tfi", fetched_tiles, tiles, preferred_element_type=jnp.float32
    )
    block_range = jnp.arange(n_blocks, dtype=jnp.int32)
    row_hot = (row_local[:, None] == block_range[None, :]).astype(jnp.float32)
    local_sum = jnp.einsum("tfi,tb->fbi", forward_terms, row_hot, precision=lax.Precision.HIGHEST)
    in_hot = (block_ids.reshape(-1)[:, None] == block_range[None, :]).astype(jnp.bfloat16)
    mirror_sum = jnp.einsum(
        "sk,sb->bk",
        incoming.reshape(n_row * capacity, feat_q * tile_dim),
        in_hot,
        preferred_element_type=jnp.float32,
    )
    mirror_sum = mirror_sum.reshape(n_blocks, feat_q, tile_dim).transpose(1, 0, 2)
    z_part = (local_sum + mirror_sum).reshape(feat_q, rows).astype(jnp.bfloat16)
    z_full = gather_groups(z_part, n_col)
    y_full = lax.dot_general(
        z_full, weight, (((0,), (0,)), ((), ())), preferred_element_type=jnp.float32
    )
    act = jax.nn.silu(y_full).astype(jnp.bfloat16)
    sig = jax.nn.sigmoid(y_full)
    grad_y = (cotangent.astype(jnp.float32) * sig * (1.0 + y_full * (1.0 - sig))).astype(
        jnp.bfloat16
    )
    grad_part = jnp.dot(z_part, grad_y, preferred_element_type=jnp.float32)
    grad_w = sum_over_row(grad_part, n_row)
    return (act, grad_w)


def solution(mesh):
    in_specs = (
        P("col", "row"),
        P("row", None, None),
        P("row", None),
        P("row", None),
        P(),
        P("row", None),
    )
    out_specs = (P("row", None), P("col", None))
    return jax.shard_map(body, mesh=mesh, in_specs=in_specs, out_specs=out_specs, check_vma=False)
```

```python
import jax
import jax.numpy as jnp
from jax import lax
from jax.sharding import PartitionSpec as P


def rows_of(a, idx):
    return a.at[idx].get(mode="promise_in_bounds")


def gather_groups(z_part, n_col):
    if n_col == 1:
        return z_part
    me = lax.axis_index("col")
    if n_col & (n_col - 1):
        parts = [z_part]
        for k in range(1, n_col):
            perm = [(i, (i + k) % n_col) for i in range(n_col)]
            parts.append(lax.ppermute(z_part, "col", perm))
        order = (me - jnp.arange(n_col, dtype=jnp.int32)) % n_col
        full = rows_of(jnp.stack(parts), order)
        return full.reshape(n_col * z_part.shape[0], z_part.shape[1])
    parts = [z_part]
    for k in range(1, n_col):
        parts.append(lax.ppermute(z_part, "col", [(i, i ^ k) for i in range(n_col)]))
    groups = []
    for j in range(n_col):
        pick = parts[n_col - 1]
        for k in range(n_col - 2, -1, -1):
            pick = jnp.where((me ^ k) == j, parts[k], pick)
        groups.append(pick)
    return jnp.concatenate(groups, axis=0)


def sum_over_row(x, n_row):
    every = jnp.broadcast_to(x[None], (n_row,) + x.shape)
    parts = lax.all_to_all(every, "row", split_axis=0, concat_axis=0, tiled=True)
    total = parts[0]
    for i in range(1, n_row):
        total = total + parts[i]
    return total


def body(x_t, tiles, tile_owner, tile_local, weight, cotangent):
    n_row = lax.axis_size("row")
    n_col = lax.axis_size("col")
    n_tiles, tile_dim = (tiles.shape[0], tiles.shape[1])
    feat_q, rows = x_t.shape
    n_blocks = rows // tile_dim
    capacity = 2 * (n_tiles // n_row)
    xb = x_t.reshape(feat_q, n_blocks, tile_dim).transpose(1, 0, 2)
    flat_blocks = xb.reshape(n_blocks, feat_q * tile_dim)
    key = (tile_owner[:, 0] * n_blocks + tile_local[:, 1]) * n_blocks + tile_local[:, 0]
    owner = key // (n_blocks * n_blocks)
    col_local = (key // n_blocks) % n_blocks
    row_local = key % n_blocks
    tile_ids = jnp.arange(n_tiles, dtype=jnp.int32)
    same = owner[:, None] == owner[None, :]
    rank = jnp.sum((same & (tile_ids[None, :] < tile_ids[:, None])).astype(jnp.int32), axis=1)
    slot = owner * capacity + rank
    slot_range = jnp.arange(n_row * capacity, dtype=jnp.int32)
    slot_hot = slot[None, :] == slot_range[:, None]
    lane_slots = jnp.broadcast_to(slot_range.reshape(n_row, capacity, 1), (n_row, capacity, 128))
    requests = jnp.sum(
        jnp.where(slot[None, None, None, :] == lane_slots[..., None], col_local[None, None, None, :], 0),
        axis=-1,
    )
    own_blocks = rows_of(xb, row_local)
    mirror_terms = jnp.einsum(
        "tfi,tij->tfj", own_blocks, tiles, preferred_element_type=jnp.float32
    ).astype(jnp.bfloat16)
    outgoing = jnp.zeros((n_row * capacity, feat_q, tile_dim), jnp.bfloat16)
    outgoing = outgoing.at[slot].set(mirror_terms, mode="promise_in_bounds", unique_indices=True)
    source = jnp.concatenate([xb, outgoing], axis=0)
    got_ids = lax.all_to_all(requests, "row", split_axis=0, concat_axis=0, tiled=True)
    block_ids = got_ids[:, :, 0]
    mirror_rows = n_blocks + slot_range.reshape(n_row, capacity)
    pick = jnp.concatenate([block_ids, mirror_rows], axis=1)
    payload = rows_of(source, pick.reshape(-1)).reshape(n_row, 2 * capacity, feat_q, tile_dim)
    both = lax.all_to_all(payload, "row", split_axis=0, concat_axis=0, tiled=True)
    fetched = both[:, :capacity].reshape(n_row * capacity, feat_q, tile_dim)
    incoming = both[:, capacity:]
    fetched_tiles = rows_of(fetched, slot)
    forward_terms = jnp.einsum(
        "tfj,tij->tfi", fetched_tiles, tiles, preferred_element_type=jnp.float32
    )
    block_range = jnp.arange(n_blocks, dtype=jnp.int32)
    row_hot = (row_local[:, None] == block_range[None, :]).astype(jnp.float32)
    local_sum = jnp.einsum("tfi,tb->fbi", forward_terms, row_hot, precision=lax.Precision.HIGHEST)
    in_hot = (block_ids.reshape(-1)[:, None] == block_range[None, :]).astype(jnp.bfloat16)
    mirror_sum = jnp.einsum(
        "sk,sb->bk",
        incoming.reshape(n_row * capacity, feat_q * tile_dim),
        in_hot,
        preferred_element_type=jnp.float32,
    )
    mirror_sum = mirror_sum.reshape(n_blocks, feat_q, tile_dim).transpose(1, 0, 2)
    z_part = (local_sum + mirror_sum).reshape(feat_q, rows).astype(jnp.bfloat16)
    z_full = gather_groups(z_part, n_col)
    y_full = lax.dot_general(
        z_full, weight, (((0,), (0,)), ((), ())), preferred_element_type=jnp.float32
    )
    act = jax.nn.silu(y_full).astype(jnp.bfloat16)
    sig = jax.nn.sigmoid(y_full)
    grad_y = (cotangent.astype(jnp.float32) * sig * (1.0 + y_full * (1.0 - sig))).astype(
        jnp.bfloat16
    )
    grad_part = jnp.dot(z_part, grad_y, preferred_element_type=jnp.float32)
    grad_w = sum_over_row(grad_part, n_row)
    return (act, grad_w)


def solution(mesh):
    in_specs = (
        P("col", "row"),
        P("row", None, None),
        P("row", None),
        P("row", None),
        P(),
        P("row", None),
    )
    out_specs = (P("row", None), P("col", None))
    return jax.shard_map(body, mesh=mesh, in_specs=in_specs, out_specs=out_specs, check_vma=False)
```

```python
import jax
import jax.numpy as jnp
from jax import lax
from jax.sharding import PartitionSpec as P


def rows_of(a, idx):
    return a.at[idx].get(mode="promise_in_bounds")


def gather_groups(z_part, n_col):
    if n_col == 1:
        return z_part
    me = lax.axis_index("col")
    if n_col & (n_col - 1):
        parts = [z_part]
        for k in range(1, n_col):
            perm = [(i, (i + k) % n_col) for i in range(n_col)]
            parts.append(lax.ppermute(z_part, "col", perm))
        order = (me - jnp.arange(n_col, dtype=jnp.int32)) % n_col
        full = rows_of(jnp.stack(parts), order)
        return full.reshape(n_col * z_part.shape[0], z_part.shape[1])
    parts = [z_part]
    for k in range(1, n_col):
        parts.append(lax.ppermute(z_part, "col", [(i, i ^ k) for i in range(n_col)]))
    groups = []
    for j in range(n_col):
        pick = parts[n_col - 1]
        for k in range(n_col - 2, -1, -1):
            pick = jnp.where((me ^ k) == j, parts[k], pick)
        groups.append(pick)
    return jnp.concatenate(groups, axis=0)


def sum_over_row(x, n_row):
    every = jnp.broadcast_to(x[None], (n_row,) + x.shape)
    parts = lax.all_to_all(every, "row", split_axis=0, concat_axis=0, tiled=True)
    total = parts[0]
    for i in range(1, n_row):
        total = total + parts[i]
    return total


def body(x_t, tiles, tile_owner, tile_local, weight, cotangent):
    n_row = lax.axis_size("row")
    n_col = lax.axis_size("col")
    n_tiles, tile_dim = (tiles.shape[0], tiles.shape[1])
    feat_q, rows = x_t.shape
    n_blocks = rows // tile_dim
    capacity = 2 * (n_tiles // n_row)
    xb = x_t.reshape(feat_q, n_blocks, tile_dim).transpose(1, 0, 2)
    flat_blocks = xb.reshape(n_blocks, feat_q * tile_dim)
    key = (tile_owner[:, 0] * n_blocks + tile_local[:, 1]) * n_blocks + tile_local[:, 0]
    owner = key // (n_blocks * n_blocks)
    col_local = (key // n_blocks) % n_blocks
    row_local = key % n_blocks
    tile_ids = jnp.arange(n_tiles, dtype=jnp.int32)
    same = owner[:, None] == owner[None, :]
    rank = jnp.sum((same & (tile_ids[None, :] < tile_ids[:, None])).astype(jnp.int32), axis=1)
    slot = owner * capacity + rank
    slot_range = jnp.arange(n_row * capacity, dtype=jnp.int32)
    slot_hot = slot[None, :] == slot_range[:, None]
    lane_slots = jnp.broadcast_to(slot_range.reshape(n_row, capacity, 1), (n_row, capacity, 128))
    requests = jnp.sum(
        jnp.where(slot[None, None, None, :] == lane_slots[..., None], col_local[None, None, None, :], 0),
        axis=-1,
    )
    own_blocks = rows_of(xb, row_local)
    mirror_terms = jnp.einsum(
        "tfi,tij->tfj", own_blocks, tiles, preferred_element_type=jnp.float32
    ).astype(jnp.bfloat16)
    outgoing = jnp.zeros((n_row * capacity, feat_q, tile_dim), jnp.bfloat16)
    outgoing = outgoing.at[slot].set(mirror_terms, mode="promise_in_bounds", unique_indices=True)
    base = jnp.concatenate(
        [jnp.zeros_like(outgoing), outgoing], axis=0
    ).reshape(2, n_row, capacity, feat_q, tile_dim).transpose(1, 0, 2, 3, 4)
    base = base.reshape(n_row, 2 * capacity, feat_q, tile_dim)
    got_ids = lax.all_to_all(requests, "row", split_axis=0, concat_axis=0, tiled=True)
    block_ids = got_ids[:, :, 0]
    asked = rows_of(xb, block_ids.reshape(-1)).reshape(n_row, capacity, feat_q, tile_dim)
    payload = lax.dynamic_update_slice(base, asked, (0, 0, 0, 0))
    both = lax.all_to_all(payload, "row", split_axis=0, concat_axis=0, tiled=True)
    fetched = both[:, :capacity].reshape(n_row * capacity, feat_q, tile_dim)
    incoming = both[:, capacity:]
    fetched_tiles = rows_of(fetched, slot)
    forward_terms = jnp.einsum(
        "tfj,tij->tfi", fetched_tiles, tiles, preferred_element_type=jnp.float32
    )
    block_range = jnp.arange(n_blocks, dtype=jnp.int32)
    row_hot = (row_local[:, None] == block_range[None, :]).astype(jnp.float32)
    local_sum = jnp.einsum("tfi,tb->fbi", forward_terms, row_hot, precision=lax.Precision.HIGHEST)
    in_hot = (block_ids.reshape(-1)[:, None] == block_range[None, :]).astype(jnp.bfloat16)
    mirror_sum = jnp.einsum(
        "sk,sb->bk",
        incoming.reshape(n_row * capacity, feat_q * tile_dim),
        in_hot,
        preferred_element_type=jnp.float32,
    )
    mirror_sum = mirror_sum.reshape(n_blocks, feat_q, tile_dim).transpose(1, 0, 2)
    z_part = (local_sum + mirror_sum).reshape(feat_q, rows).astype(jnp.bfloat16)
    z_full = gather_groups(z_part, n_col)
    y_full = lax.dot_general(
        z_full, weight, (((0,), (0,)), ((), ())), preferred_element_type=jnp.float32
    )
    act = jax.nn.silu(y_full).astype(jnp.bfloat16)
    sig = jax.nn.sigmoid(y_full)
    grad_y = (cotangent.astype(jnp.float32) * sig * (1.0 + y_full * (1.0 - sig))).astype(
        jnp.bfloat16
    )
    grad_part = jnp.dot(z_part, grad_y, preferred_element_type=jnp.float32)
    grad_w = sum_over_row(grad_part, n_row)
    return (act, grad_w)


def solution(mesh):
    in_specs = (
        P("col", "row"),
        P("row", None, None),
        P("row", None),
        P("row", None),
        P(),
        P("row", None),
    )
    out_specs = (P("row", None), P("col", None))
    return jax.shard_map(body, mesh=mesh, in_specs=in_specs, out_specs=out_specs, check_vma=False)
```

```python
import jax
import jax.numpy as jnp
from jax import lax
from jax.sharding import PartitionSpec as P


def rows_of(a, idx):
    return a.at[idx].get(mode="promise_in_bounds")


def gather_groups(z_part, n_col):
    if n_col == 1:
        return z_part
    me = lax.axis_index("col")
    if n_col & (n_col - 1):
        parts = [z_part]
        for k in range(1, n_col):
            perm = [(i, (i + k) % n_col) for i in range(n_col)]
            parts.append(lax.ppermute(z_part, "col", perm))
        order = (me - jnp.arange(n_col, dtype=jnp.int32)) % n_col
        full = rows_of(jnp.stack(parts), order)
        return full.reshape(n_col * z_part.shape[0], z_part.shape[1])
    parts = [z_part]
    for k in range(1, n_col):
        parts.append(lax.ppermute(z_part, "col", [(i, i ^ k) for i in range(n_col)]))
    groups = []
    for j in range(n_col):
        pick = parts[n_col - 1]
        for k in range(n_col - 2, -1, -1):
            pick = jnp.where((me ^ k) == j, parts[k], pick)
        groups.append(pick)
    return jnp.concatenate(groups, axis=0)


def sum_over_row(x, n_row):
    every = jnp.broadcast_to(x[None], (n_row,) + x.shape)
    parts = lax.all_to_all(every, "row", split_axis=0, concat_axis=0, tiled=True)
    total = parts[0]
    for i in range(1, n_row):
        total = total + parts[i]
    return total


def body(x_t, tiles, tile_owner, tile_local, weight, cotangent):
    n_row = lax.axis_size("row")
    n_col = lax.axis_size("col")
    n_tiles, tile_dim = (tiles.shape[0], tiles.shape[1])
    feat_q, rows = x_t.shape
    n_blocks = rows // tile_dim
    capacity = 2 * (n_tiles // n_row)
    xb = x_t.reshape(feat_q, n_blocks, tile_dim).transpose(1, 0, 2)
    flat_blocks = xb.reshape(n_blocks, feat_q * tile_dim)
    key = (tile_owner[:, 0] * n_blocks + tile_local[:, 1]) * n_blocks + tile_local[:, 0]
    owner = key // (n_blocks * n_blocks)
    col_local = (key // n_blocks) % n_blocks
    row_local = key % n_blocks
    tile_ids = jnp.arange(n_tiles, dtype=jnp.int32)
    same = owner[:, None] == owner[None, :]
    rank = jnp.sum((same & (tile_ids[None, :] < tile_ids[:, None])).astype(jnp.int32), axis=1)
    slot = owner * capacity + rank
    slot_range = jnp.arange(n_row * capacity, dtype=jnp.int32)
    slot_hot = slot[None, :] == slot_range[:, None]
    lane_slots = jnp.broadcast_to(slot_range.reshape(n_row, capacity, 1), (n_row, capacity, 128))
    requests = jnp.sum(
        jnp.where(slot[None, None, None, :] == lane_slots[..., None], col_local[None, None, None, :], 0),
        axis=-1,
    )
    own_blocks = rows_of(xb, row_local)
    mirror_terms = jnp.einsum(
        "tfi,tij->tfj", own_blocks, tiles, preferred_element_type=jnp.float32
    ).astype(jnp.bfloat16)
    outgoing = jnp.zeros((n_row * capacity, feat_q, tile_dim), jnp.bfloat16)
    outgoing = outgoing.at[slot].set(mirror_terms, mode="promise_in_bounds", unique_indices=True)
    base = jnp.concatenate(
        [jnp.zeros_like(outgoing), outgoing], axis=0
    ).reshape(2, n_row, capacity, feat_q, tile_dim).transpose(1, 0, 2, 3, 4)
    base = base.reshape(n_row, 2 * capacity, feat_q, tile_dim)
    got_ids = lax.all_to_all(requests, "row", split_axis=0, concat_axis=0, tiled=True)
    block_ids = got_ids[:, :, 0]
    asked = rows_of(xb, block_ids.reshape(-1)).reshape(n_row, capacity, feat_q, tile_dim)
    payload = lax.dynamic_update_slice(base, asked, (0, 0, 0, 0))
    both = lax.all_to_all(payload, "row", split_axis=0, concat_axis=0, tiled=True)
    fetched = both[:, :capacity].reshape(n_row * capacity, feat_q, tile_dim)
    incoming = both[:, capacity:].reshape(n_row * capacity, feat_q, tile_dim)
    tile_of_slot = jnp.sum(jnp.where(slot_hot, tile_ids[None, :], 0), axis=1)
    slot_used = jnp.any(slot_hot, axis=1)
    tiles_by_slot = jnp.where(slot_used[:, None, None], rows_of(tiles, tile_of_slot), 0)
    row_of_slot = jnp.where(slot_used, rows_of(row_local, tile_of_slot), -1)
    forward_terms = jnp.einsum(
        "sfj,sij->sfi", fetched, tiles_by_slot, preferred_element_type=jnp.float32
    )
    block_range = jnp.arange(n_blocks, dtype=jnp.int32)
    terms = jnp.concatenate([forward_terms, incoming.astype(jnp.float32)], axis=0)
    targets = jnp.concatenate([row_of_slot, block_ids.reshape(-1)], axis=0)
    target_hot = (targets[:, None] == block_range[None, :]).astype(jnp.float32)
    z_sum = jnp.einsum("sfi,sb->fbi", terms, target_hot, precision=lax.Precision.HIGHEST)
    z_part = z_sum.reshape(feat_q, rows).astype(jnp.bfloat16)
    z_full = gather_groups(z_part, n_col)
    y_full = lax.dot_general(
        z_full, weight, (((0,), (0,)), ((), ())), preferred_element_type=jnp.float32
    )
    act = jax.nn.silu(y_full).astype(jnp.bfloat16)
    sig = jax.nn.sigmoid(y_full)
    grad_y = (cotangent.astype(jnp.float32) * sig * (1.0 + y_full * (1.0 - sig))).astype(
        jnp.bfloat16
    )
    grad_part = jnp.dot(z_part, grad_y, preferred_element_type=jnp.float32)
    grad_w = sum_over_row(grad_part, n_row)
    return (act, grad_w)


def solution(mesh):
    in_specs = (
        P("col", "row"),
        P("row", None, None),
        P("row", None),
        P("row", None),
        P(),
        P("row", None),
    )
    out_specs = (P("row", None), P("col", None))
    return jax.shard_map(body, mesh=mesh, in_specs=in_specs, out_specs=out_specs, check_vma=False)
```

```python
import jax
import jax.numpy as jnp
from jax import lax
from jax.sharding import PartitionSpec as P


def rows_of(a, idx):
    return a.at[idx].get(mode="promise_in_bounds")


def gather_groups(z_part, n_col):
    if n_col == 1:
        return z_part
    me = lax.axis_index("col")
    if n_col & (n_col - 1):
        parts = [z_part]
        for k in range(1, n_col):
            perm = [(i, (i + k) % n_col) for i in range(n_col)]
            parts.append(lax.ppermute(z_part, "col", perm))
        order = (me - jnp.arange(n_col, dtype=jnp.int32)) % n_col
        full = rows_of(jnp.stack(parts), order)
        return full.reshape(n_col * z_part.shape[0], z_part.shape[1])
    parts = [z_part]
    for k in range(1, n_col):
        parts.append(lax.ppermute(z_part, "col", [(i, i ^ k) for i in range(n_col)]))
    groups = []
    for j in range(n_col):
        pick = parts[n_col - 1]
        for k in range(n_col - 2, -1, -1):
            pick = jnp.where((me ^ k) == j, parts[k], pick)
        groups.append(pick)
    return jnp.concatenate(groups, axis=0)


def sum_over_row(x, n_row):
    every = jnp.broadcast_to(x[None], (n_row,) + x.shape)
    parts = lax.all_to_all(every, "row", split_axis=0, concat_axis=0, tiled=True)
    total = parts[0]
    for i in range(1, n_row):
        total = total + parts[i]
    return total


def body(x_t, tiles, tile_owner, tile_local, weight, cotangent):
    n_row = lax.axis_size("row")
    n_col = lax.axis_size("col")
    n_tiles, tile_dim = (tiles.shape[0], tiles.shape[1])
    feat_q, rows = x_t.shape
    n_blocks = rows // tile_dim
    capacity = 2 * (n_tiles // n_row)
    xb = x_t.reshape(feat_q, n_blocks, tile_dim).transpose(1, 0, 2)
    flat_blocks = xb.reshape(n_blocks, feat_q * tile_dim)
    key = (tile_owner[:, 0] * n_blocks + tile_local[:, 1]) * n_blocks + tile_local[:, 0]
    owner = key // (n_blocks * n_blocks)
    col_local = (key // n_blocks) % n_blocks
    row_local = key % n_blocks
    if n_col > 1:
        late_local = lax.ppermute(tile_local, "col", [(i, i ^ 1) for i in range(n_col)])
    else:
        late_local = tile_local
    tile_ids = jnp.arange(n_tiles, dtype=jnp.int32)
    same = owner[:, None] == owner[None, :]
    rank = jnp.sum((same & (tile_ids[None, :] < tile_ids[:, None])).astype(jnp.int32), axis=1)
    slot = owner * capacity + rank
    slot_range = jnp.arange(n_row * capacity, dtype=jnp.int32)
    slot_hot = slot[None, :] == slot_range[:, None]
    lane_slots = jnp.broadcast_to(slot_range.reshape(n_row, capacity, 1), (n_row, capacity, 128))
    requests = jnp.sum(
        jnp.where(slot[None, None, None, :] == lane_slots[..., None], col_local[None, None, None, :], 0),
        axis=-1,
    )
    own_blocks = rows_of(xb, row_local)
    mirror_terms = jnp.einsum(
        "tfi,tij->tfj", own_blocks, tiles, preferred_element_type=jnp.float32
    ).astype(jnp.bfloat16)
    outgoing = jnp.zeros((n_row * capacity, feat_q, tile_dim), jnp.bfloat16)
    outgoing = outgoing.at[slot].set(mirror_terms, mode="promise_in_bounds", unique_indices=True)
    base = jnp.concatenate(
        [jnp.zeros_like(outgoing), outgoing], axis=0
    ).reshape(2, n_row, capacity, feat_q, tile_dim).transpose(1, 0, 2, 3, 4)
    base = base.reshape(n_row, 2 * capacity, feat_q, tile_dim)
    got_ids = lax.all_to_all(requests, "row", split_axis=0, concat_axis=0, tiled=True)
    block_ids = got_ids[:, :, 0]
    asked = rows_of(xb, block_ids.reshape(-1)).reshape(n_row, capacity, feat_q, tile_dim)
    payload = lax.dynamic_update_slice(base, asked, (0, 0, 0, 0))
    both = lax.all_to_all(payload, "row", split_axis=0, concat_axis=0, tiled=True)
    fetched = both[:, :capacity].reshape(n_row * capacity, feat_q, tile_dim)
    incoming = both[:, capacity:].reshape(n_row * capacity, feat_q, tile_dim)
    tile_of_slot = jnp.sum(jnp.where(slot_hot, tile_ids[None, :], 0), axis=1)
    slot_used = jnp.any(slot_hot, axis=1)
    tiles_by_slot = jnp.where(slot_used[:, None, None], rows_of(tiles, tile_of_slot), 0)
    row_of_slot = jnp.where(slot_used, rows_of(late_local[:, 0], tile_of_slot), -1)
    forward_terms = jnp.einsum(
        "sfj,sij->sfi", fetched, tiles_by_slot, preferred_element_type=jnp.float32
    )
    block_range = jnp.arange(n_blocks, dtype=jnp.int32)
    terms = jnp.concatenate([forward_terms, incoming.astype(jnp.float32)], axis=0)
    targets = jnp.concatenate([row_of_slot, block_ids.reshape(-1)], axis=0)
    target_hot = (targets[:, None] == block_range[None, :]).astype(jnp.float32)
    z_sum = jnp.einsum("sfi,sb->fbi", terms, target_hot, precision=lax.Precision.HIGHEST)
    z_part = z_sum.reshape(feat_q, rows).astype(jnp.bfloat16)
    z_full = gather_groups(z_part, n_col)
    y_full = lax.dot_general(
        z_full, weight, (((0,), (0,)), ((), ())), preferred_element_type=jnp.float32
    )
    act = jax.nn.silu(y_full).astype(jnp.bfloat16)
    sig = jax.nn.sigmoid(y_full)
    grad_y = (cotangent.astype(jnp.float32) * sig * (1.0 + y_full * (1.0 - sig))).astype(
        jnp.bfloat16
    )
    grad_part = jnp.dot(z_part, grad_y, preferred_element_type=jnp.float32)
    grad_w = sum_over_row(grad_part, n_row)
    return (act, grad_w)


def solution(mesh):
    in_specs = (
        P("col", "row"),
        P("row", None, None),
        P("row", None),
        P("row", None),
        P(),
        P("row", None),
    )
    out_specs = (P("row", None), P("col", None))
    return jax.shard_map(body, mesh=mesh, in_specs=in_specs, out_specs=out_specs, check_vma=False)
```

```python
import jax
import jax.numpy as jnp
from jax import lax
from jax.experimental import pallas as pl
from jax.experimental.pallas import tpu as pltpu
from jax.sharding import PartitionSpec as P


def rows_of(a, idx):
    return a.at[idx].get(mode="promise_in_bounds")


def gather_groups(z_part, n_col):
    if n_col == 1:
        return z_part
    me = lax.axis_index("col")
    if n_col & (n_col - 1):
        parts = [z_part]
        for k in range(1, n_col):
            perm = [(i, (i + k) % n_col) for i in range(n_col)]
            parts.append(lax.ppermute(z_part, "col", perm))
        order = (me - jnp.arange(n_col, dtype=jnp.int32)) % n_col
        full = rows_of(jnp.stack(parts), order)
        return full.reshape(n_col * z_part.shape[0], z_part.shape[1])
    parts = [z_part]
    for k in range(1, n_col):
        parts.append(lax.ppermute(z_part, "col", [(i, i ^ k) for i in range(n_col)]))
    groups = []
    for j in range(n_col):
        pick = parts[n_col - 1]
        for k in range(n_col - 2, -1, -1):
            pick = jnp.where((me ^ k) == j, parts[k], pick)
        groups.append(pick)
    return jnp.concatenate(groups, axis=0)


def sum_over_row(x, n_row):
    every = jnp.broadcast_to(x[None], (n_row,) + x.shape)
    parts = lax.all_to_all(every, "row", split_axis=0, concat_axis=0, tiled=True)
    total = parts[0]
    for i in range(1, n_row):
        total = total + parts[i]
    return total


def tail_kernel(z_full_ref, w_ref, cot_ref, z_part_ref, act_ref, grad_ref):
    y = lax.dot_general(
        z_full_ref[...], w_ref[...], (((0,), (0,)), ((), ())), preferred_element_type=jnp.float32
    )
    sig = 1.0 / (1.0 + jnp.exp(-y))
    act_ref[...] = (y * sig).astype(act_ref.dtype)
    grad_y = (cot_ref[...].astype(jnp.float32) * sig * (1.0 + y * (1.0 - sig))).astype(jnp.bfloat16)
    grad_ref[...] = jnp.dot(z_part_ref[...], grad_y, preferred_element_type=jnp.float32)


def layer_tail(z_full, weight, cotangent, z_part):
    nodes, hid = cotangent.shape
    feat, feat_q = z_full.shape[0], z_part.shape[0]
    flops = 2 * nodes * hid * (feat + feat_q) + 12 * nodes * hid
    nbytes = 2 * (z_full.size + weight.size + cotangent.size + z_part.size + nodes * hid) + 4 * feat_q * hid
    vmem = pl.BlockSpec(memory_space=pltpu.VMEM)
    return pl.pallas_call(
        tail_kernel,
        out_shape=(
            jax.ShapeDtypeStruct((nodes, hid), jnp.bfloat16),
            jax.ShapeDtypeStruct((feat_q, hid), jnp.float32),
        ),
        in_specs=[vmem] * 4,
        out_specs=(vmem, vmem),
        cost_estimate=pl.CostEstimate(flops=flops, transcendentals=nodes * hid, bytes_accessed=nbytes),
    )(z_full, weight, cotangent, z_part)


def body(x_t, tiles, tile_owner, tile_local, weight, cotangent):
    n_row = lax.axis_size("row")
    n_col = lax.axis_size("col")
    n_tiles, tile_dim = (tiles.shape[0], tiles.shape[1])
    feat_q, rows = x_t.shape
    n_blocks = rows // tile_dim
    capacity = 2 * (n_tiles // n_row)
    xb = x_t.reshape(feat_q, n_blocks, tile_dim).transpose(1, 0, 2)
    flat_blocks = xb.reshape(n_blocks, feat_q * tile_dim)
    key = (tile_owner[:, 0] * n_blocks + tile_local[:, 1]) * n_blocks + tile_local[:, 0]
    owner = key // (n_blocks * n_blocks)
    col_local = (key // n_blocks) % n_blocks
    row_local = key % n_blocks
    tile_ids = jnp.arange(n_tiles, dtype=jnp.int32)
    same = owner[:, None] == owner[None, :]
    rank = jnp.sum((same & (tile_ids[None, :] < tile_ids[:, None])).astype(jnp.int32), axis=1)
    slot = owner * capacity + rank
    slot_range = jnp.arange(n_row * capacity, dtype=jnp.int32)
    slot_hot = slot[None, :] == slot_range[:, None]
    lane_slots = jnp.broadcast_to(slot_range.reshape(n_row, capacity, 1), (n_row, capacity, 128))
    requests = jnp.sum(
        jnp.where(slot[None, None, None, :] == lane_slots[..., None], col_local[None, None, None, :], 0),
        axis=-1,
    )
    own_blocks = rows_of(xb, row_local)
    mirror_terms = jnp.einsum(
        "tfi,tij->tfj", own_blocks, tiles, preferred_element_type=jnp.float32
    ).astype(jnp.bfloat16)
    outgoing = jnp.zeros((n_row * capacity, feat_q, tile_dim), jnp.bfloat16)
    outgoing = outgoing.at[slot].set(mirror_terms, mode="promise_in_bounds", unique_indices=True)
    base = jnp.concatenate(
        [jnp.zeros_like(outgoing), outgoing], axis=0
    ).reshape(2, n_row, capacity, feat_q, tile_dim).transpose(1, 0, 2, 3, 4)
    base = base.reshape(n_row, 2 * capacity, feat_q, tile_dim)
    got_ids = lax.all_to_all(requests, "row", split_axis=0, concat_axis=0, tiled=True)
    block_ids = got_ids[:, :, 0]
    asked = rows_of(xb, block_ids.reshape(-1)).reshape(n_row, capacity, feat_q, tile_dim)
    payload = lax.dynamic_update_slice(base, asked, (0, 0, 0, 0))
    both = lax.all_to_all(payload, "row", split_axis=0, concat_axis=0, tiled=True)
    fetched = both[:, :capacity].reshape(n_row * capacity, feat_q, tile_dim)
    incoming = both[:, capacity:].reshape(n_row * capacity, feat_q, tile_dim)
    tile_of_slot = jnp.sum(jnp.where(slot_hot, tile_ids[None, :], 0), axis=1)
    slot_used = jnp.any(slot_hot, axis=1)
    tiles_by_slot = jnp.where(slot_used[:, None, None], rows_of(tiles, tile_of_slot), 0)
    row_of_slot = jnp.where(slot_used, rows_of(row_local, tile_of_slot), -1)
    forward_terms = jnp.einsum(
        "sfj,sij->sfi", fetched, tiles_by_slot, preferred_element_type=jnp.float32
    )
    block_range = jnp.arange(n_blocks, dtype=jnp.int32)
    terms = jnp.concatenate([forward_terms, incoming.astype(jnp.float32)], axis=0)
    targets = jnp.concatenate([row_of_slot, block_ids.reshape(-1)], axis=0)
    target_hot = (targets[:, None] == block_range[None, :]).astype(jnp.float32)
    z_sum = jnp.einsum("sfi,sb->fbi", terms, target_hot, precision=lax.Precision.HIGHEST)
    z_part = z_sum.reshape(feat_q, rows).astype(jnp.bfloat16)
    z_full = gather_groups(z_part, n_col)
    act, grad_part = layer_tail(z_full, weight, cotangent, z_part)
    grad_w = sum_over_row(grad_part, n_row)
    return (act, grad_w)


def solution(mesh):
    in_specs = (
        P("col", "row"),
        P("row", None, None),
        P("row", None),
        P("row", None),
        P(),
        P("row", None),
    )
    out_specs = (P("row", None), P("col", None))
    return jax.shard_map(body, mesh=mesh, in_specs=in_specs, out_specs=out_specs, check_vma=False)
```

```python
import jax
import jax.numpy as jnp
from jax import lax
from jax.sharding import PartitionSpec as P


def rows_of(a, idx):
    return a.at[idx].get(mode="promise_in_bounds")


def gather_groups(z_part, n_col):
    if n_col == 1:
        return z_part
    me = lax.axis_index("col")
    if n_col & (n_col - 1):
        parts = [z_part]
        for k in range(1, n_col):
            perm = [(i, (i + k) % n_col) for i in range(n_col)]
            parts.append(lax.ppermute(z_part, "col", perm))
        order = (me - jnp.arange(n_col, dtype=jnp.int32)) % n_col
        full = rows_of(jnp.stack(parts), order)
        return full.reshape(n_col * z_part.shape[0], z_part.shape[1])
    if n_col == 4:
        across = lax.ppermute(z_part, "col", [(i, i ^ 2) for i in range(n_col)])
        beside = lax.ppermute(z_part, "col", [(i, i ^ 1) for i in range(n_col)])
        corner = lax.ppermute(across, "col", [(i, i ^ 1) for i in range(n_col)])
        parts = [z_part, beside, across, corner]
    else:
        parts = [z_part]
        for k in range(1, n_col):
            parts.append(lax.ppermute(z_part, "col", [(i, i ^ k) for i in range(n_col)]))
    groups = []
    for j in range(n_col):
        pick = parts[n_col - 1]
        for k in range(n_col - 2, -1, -1):
            pick = jnp.where((me ^ k) == j, parts[k], pick)
        groups.append(pick)
    return jnp.concatenate(groups, axis=0)


def sum_over_row(x, n_row):
    every = jnp.broadcast_to(x[None], (n_row,) + x.shape)
    parts = lax.all_to_all(every, "row", split_axis=0, concat_axis=0, tiled=True)
    total = parts[0]
    for i in range(1, n_row):
        total = total + parts[i]
    return total


def body(x_t, tiles, tile_owner, tile_local, weight, cotangent):
    n_row = lax.axis_size("row")
    n_col = lax.axis_size("col")
    n_tiles, tile_dim = (tiles.shape[0], tiles.shape[1])
    feat_q, rows = x_t.shape
    n_blocks = rows // tile_dim
    capacity = 2 * (n_tiles // n_row)
    xb = x_t.reshape(feat_q, n_blocks, tile_dim).transpose(1, 0, 2)
    flat_blocks = xb.reshape(n_blocks, feat_q * tile_dim)
    key = (tile_owner[:, 0] * n_blocks + tile_local[:, 1]) * n_blocks + tile_local[:, 0]
    owner = key // (n_blocks * n_blocks)
    col_local = (key // n_blocks) % n_blocks
    row_local = key % n_blocks
    tile_ids = jnp.arange(n_tiles, dtype=jnp.int32)
    same = owner[:, None] == owner[None, :]
    rank = jnp.sum((same & (tile_ids[None, :] < tile_ids[:, None])).astype(jnp.int32), axis=1)
    slot = owner * capacity + rank
    slot_range = jnp.arange(n_row * capacity, dtype=jnp.int32)
    slot_hot = slot[None, :] == slot_range[:, None]
    lane_slots = jnp.broadcast_to(slot_range.reshape(n_row, capacity, 1), (n_row, capacity, 128))
    requests = jnp.sum(
        jnp.where(slot[None, None, None, :] == lane_slots[..., None], col_local[None, None, None, :], 0),
        axis=-1,
    )
    own_blocks = rows_of(xb, row_local)
    mirror_terms = jnp.einsum(
        "tfi,tij->tfj", own_blocks, tiles, preferred_element_type=jnp.float32
    ).astype(jnp.bfloat16)
    outgoing = jnp.zeros((n_row * capacity, feat_q, tile_dim), jnp.bfloat16)
    outgoing = outgoing.at[slot].set(mirror_terms, mode="promise_in_bounds", unique_indices=True)
    base = jnp.concatenate(
        [jnp.zeros_like(outgoing), outgoing], axis=0
    ).reshape(2, n_row, capacity, feat_q, tile_dim).transpose(1, 0, 2, 3, 4)
    base = base.reshape(n_row, 2 * capacity, feat_q, tile_dim)
    got_ids = lax.all_to_all(requests, "row", split_axis=0, concat_axis=0, tiled=True)
    block_ids = got_ids[:, :, 0]
    asked = rows_of(xb, block_ids.reshape(-1)).reshape(n_row, capacity, feat_q, tile_dim)
    payload = lax.dynamic_update_slice(base, asked, (0, 0, 0, 0))
    both = lax.all_to_all(payload, "row", split_axis=0, concat_axis=0, tiled=True)
    fetched = both[:, :capacity].reshape(n_row * capacity, feat_q, tile_dim)
    incoming = both[:, capacity:].reshape(n_row * capacity, feat_q, tile_dim)
    tile_of_slot = jnp.sum(jnp.where(slot_hot, tile_ids[None, :], 0), axis=1)
    slot_used = jnp.any(slot_hot, axis=1)
    tiles_by_slot = jnp.where(slot_used[:, None, None], rows_of(tiles, tile_of_slot), 0)
    row_of_slot = jnp.where(slot_used, rows_of(row_local, tile_of_slot), -1)
    forward_terms = jnp.einsum(
        "sfj,sij->sfi", fetched, tiles_by_slot, preferred_element_type=jnp.float32
    )
    block_range = jnp.arange(n_blocks, dtype=jnp.int32)
    terms = jnp.concatenate([forward_terms, incoming.astype(jnp.float32)], axis=0)
    targets = jnp.concatenate([row_of_slot, block_ids.reshape(-1)], axis=0)
    target_hot = (targets[:, None] == block_range[None, :]).astype(jnp.float32)
    z_sum = jnp.einsum("sfi,sb->fbi", terms, target_hot, precision=lax.Precision.HIGHEST)
    z_part = z_sum.reshape(feat_q, rows).astype(jnp.bfloat16)
    z_full = gather_groups(z_part, n_col)
    y_full = lax.dot_general(
        z_full, weight, (((0,), (0,)), ((), ())), preferred_element_type=jnp.float32
    )
    act = jax.nn.silu(y_full).astype(jnp.bfloat16)
    sig = jax.nn.sigmoid(y_full)
    grad_y = (cotangent.astype(jnp.float32) * sig * (1.0 + y_full * (1.0 - sig))).astype(
        jnp.bfloat16
    )
    grad_part = jnp.dot(z_part, grad_y, preferred_element_type=jnp.float32)
    grad_w = sum_over_row(grad_part, n_row)
    return (act, grad_w)


def solution(mesh):
    in_specs = (
        P("col", "row"),
        P("row", None, None),
        P("row", None),
        P("row", None),
        P(),
        P("row", None),
    )
    out_specs = (P("row", None), P("col", None))
    return jax.shard_map(body, mesh=mesh, in_specs=in_specs, out_specs=out_specs, check_vma=False)
```

```python
import jax
import jax.numpy as jnp
from jax import lax
from jax.sharding import PartitionSpec as P


def rows_of(a, idx):
    return a.at[idx].get(mode="promise_in_bounds")


def gather_groups(z_part, n_col):
    if n_col == 1:
        return z_part
    me = lax.axis_index("col")
    if n_col & (n_col - 1):
        parts = [z_part]
        for k in range(1, n_col):
            perm = [(i, (i + k) % n_col) for i in range(n_col)]
            parts.append(lax.ppermute(z_part, "col", perm))
        order = (me - jnp.arange(n_col, dtype=jnp.int32)) % n_col
        full = rows_of(jnp.stack(parts), order)
        return full.reshape(n_col * z_part.shape[0], z_part.shape[1])
    if n_col == 4:
        across = lax.ppermute(z_part, "col", [(i, i ^ 2) for i in range(n_col)])
        beside = lax.ppermute(z_part, "col", [(i, i ^ 1) for i in range(n_col)])
        corner = lax.ppermute(across, "col", [(i, i ^ 1) for i in range(n_col)])
        parts = [z_part, beside, across, corner]
    else:
        parts = [z_part]
        for k in range(1, n_col):
            parts.append(lax.ppermute(z_part, "col", [(i, i ^ k) for i in range(n_col)]))
    groups = []
    for j in range(n_col):
        pick = parts[n_col - 1]
        for k in range(n_col - 2, -1, -1):
            pick = jnp.where((me ^ k) == j, parts[k], pick)
        groups.append(pick)
    return jnp.concatenate(groups, axis=0)


def sum_over_row(x, n_row):
    every = jnp.broadcast_to(x[None], (n_row,) + x.shape)
    parts = lax.all_to_all(every, "row", split_axis=0, concat_axis=0, tiled=True)
    total = parts[0]
    for i in range(1, n_row):
        total = total + parts[i]
    return total


def body(x_t, tiles, tile_owner, tile_local, weight, cotangent):
    n_row = lax.axis_size("row")
    n_col = lax.axis_size("col")
    n_tiles, tile_dim = (tiles.shape[0], tiles.shape[1])
    feat_q, rows = x_t.shape
    n_blocks = rows // tile_dim
    capacity = 2 * (n_tiles // n_row)
    xb = x_t.reshape(feat_q, n_blocks, tile_dim).transpose(1, 0, 2)
    flat_blocks = xb.reshape(n_blocks, feat_q * tile_dim)
    key = (tile_owner[:, 0] * n_blocks + tile_local[:, 1]) * n_blocks + tile_local[:, 0]
    owner = key // (n_blocks * n_blocks)
    col_local = (key // n_blocks) % n_blocks
    row_local = key % n_blocks
    tile_ids = jnp.arange(n_tiles, dtype=jnp.int32)
    same = owner[:, None] == owner[None, :]
    rank = jnp.sum((same & (tile_ids[None, :] < tile_ids[:, None])).astype(jnp.int32), axis=1)
    slot = owner * capacity + rank
    slot_range = jnp.arange(n_row * capacity, dtype=jnp.int32)
    slot_hot = slot[None, :] == slot_range[:, None]
    pad_rows = 8
    row_slot = jnp.arange(n_row * pad_rows, dtype=jnp.int32)
    row_slot = (row_slot // pad_rows) * capacity + row_slot % pad_rows
    row_used = (jnp.arange(n_row * pad_rows, dtype=jnp.int32) % pad_rows) < capacity
    pick_hot = ((slot[None, :] == row_slot[:, None]) & row_used[:, None]).astype(jnp.bfloat16)
    lane_local = jnp.broadcast_to(col_local[:, None], (n_tiles, 128)).astype(jnp.bfloat16)
    requests = jnp.dot(pick_hot, lane_local, preferred_element_type=jnp.float32).astype(jnp.int32)
    requests = requests.reshape(n_row, pad_rows, 128)
    own_blocks = rows_of(xb, row_local)
    mirror_terms = jnp.einsum(
        "tfi,tij->tfj", own_blocks, tiles, preferred_element_type=jnp.float32
    ).astype(jnp.bfloat16)
    outgoing = jnp.zeros((n_row * capacity, feat_q, tile_dim), jnp.bfloat16)
    outgoing = outgoing.at[slot].set(mirror_terms, mode="promise_in_bounds", unique_indices=True)
    base = jnp.concatenate(
        [jnp.zeros_like(outgoing), outgoing], axis=0
    ).reshape(2, n_row, capacity, feat_q, tile_dim).transpose(1, 0, 2, 3, 4)
    base = base.reshape(n_row, 2 * capacity, feat_q, tile_dim)
    got_ids = lax.all_to_all(requests, "row", split_axis=0, concat_axis=0, tiled=True)
    block_ids = got_ids[:, :capacity, 0]
    asked = rows_of(xb, block_ids.reshape(-1)).reshape(n_row, capacity, feat_q, tile_dim)
    payload = lax.dynamic_update_slice(base, asked, (0, 0, 0, 0))
    both = lax.all_to_all(payload, "row", split_axis=0, concat_axis=0, tiled=True)
    fetched = both[:, :capacity].reshape(n_row * capacity, feat_q, tile_dim)
    incoming = both[:, capacity:].reshape(n_row * capacity, feat_q, tile_dim)
    tile_of_slot = jnp.sum(jnp.where(slot_hot, tile_ids[None, :], 0), axis=1)
    slot_used = jnp.any(slot_hot, axis=1)
    tiles_by_slot = jnp.where(slot_used[:, None, None], rows_of(tiles, tile_of_slot), 0)
    row_of_slot = jnp.where(slot_used, rows_of(row_local, tile_of_slot), -1)
    forward_terms = jnp.einsum(
        "sfj,sij->sfi", fetched, tiles_by_slot, preferred_element_type=jnp.float32
    )
    block_range = jnp.arange(n_blocks, dtype=jnp.int32)
    terms = jnp.concatenate([forward_terms, incoming.astype(jnp.float32)], axis=0)
    targets = jnp.concatenate([row_of_slot, block_ids.reshape(-1)], axis=0)
    target_hot = (targets[:, None] == block_range[None, :]).astype(jnp.float32)
    z_sum = jnp.einsum("sfi,sb->fbi", terms, target_hot, precision=lax.Precision.HIGHEST)
    z_part = z_sum.reshape(feat_q, rows).astype(jnp.bfloat16)
    z_full = gather_groups(z_part, n_col)
    y_full = lax.dot_general(
        z_full, weight, (((0,), (0,)), ((), ())), preferred_element_type=jnp.float32
    )
    act = jax.nn.silu(y_full).astype(jnp.bfloat16)
    sig = jax.nn.sigmoid(y_full)
    grad_y = (cotangent.astype(jnp.float32) * sig * (1.0 + y_full * (1.0 - sig))).astype(
        jnp.bfloat16
    )
    grad_part = jnp.dot(z_part, grad_y, preferred_element_type=jnp.float32)
    grad_w = sum_over_row(grad_part, n_row)
    return (act, grad_w)


def solution(mesh):
    in_specs = (
        P("col", "row"),
        P("row", None, None),
        P("row", None),
        P("row", None),
        P(),
        P("row", None),
    )
    out_specs = (P("row", None), P("col", None))
    return jax.shard_map(body, mesh=mesh, in_specs=in_specs, out_specs=out_specs, check_vma=False)
```

```python
import jax
import jax.numpy as jnp
from jax import lax
from jax.sharding import PartitionSpec as P


def rows_of(a, idx):
    return a.at[idx].get(mode="promise_in_bounds")


def gather_groups(z_part, n_col):
    if n_col == 1:
        return z_part
    me = lax.axis_index("col")
    if n_col & (n_col - 1):
        parts = [z_part]
        for k in range(1, n_col):
            perm = [(i, (i + k) % n_col) for i in range(n_col)]
            parts.append(lax.ppermute(z_part, "col", perm))
        order = (me - jnp.arange(n_col, dtype=jnp.int32)) % n_col
        full = rows_of(jnp.stack(parts), order)
        return full.reshape(n_col * z_part.shape[0], z_part.shape[1])
    if n_col == 4:
        across = lax.ppermute(z_part, "col", [(i, i ^ 2) for i in range(n_col)])
        beside = lax.ppermute(z_part, "col", [(i, i ^ 1) for i in range(n_col)])
        corner = lax.ppermute(across, "col", [(i, i ^ 1) for i in range(n_col)])
        parts = [z_part, beside, across, corner]
    else:
        parts = [z_part]
        for k in range(1, n_col):
            parts.append(lax.ppermute(z_part, "col", [(i, i ^ k) for i in range(n_col)]))
    groups = []
    for j in range(n_col):
        pick = parts[n_col - 1]
        for k in range(n_col - 2, -1, -1):
            pick = jnp.where((me ^ k) == j, parts[k], pick)
        groups.append(pick)
    return jnp.concatenate(groups, axis=0)


def sum_over_row(x, n_row):
    every = jnp.broadcast_to(x[None], (n_row,) + x.shape)
    parts = lax.all_to_all(every, "row", split_axis=0, concat_axis=0, tiled=True)
    total = parts[0]
    for i in range(1, n_row):
        total = total + parts[i]
    return total


def body(x_t, tiles, tile_owner, tile_local, weight, cotangent):
    n_row = lax.axis_size("row")
    n_col = lax.axis_size("col")
    n_tiles, tile_dim = (tiles.shape[0], tiles.shape[1])
    feat_q, rows = x_t.shape
    n_blocks = rows // tile_dim
    capacity = 2 * (n_tiles // n_row)
    xb = x_t.reshape(feat_q, n_blocks, tile_dim).transpose(1, 0, 2)
    flat_blocks = xb.reshape(n_blocks, feat_q * tile_dim)
    key = (tile_owner[:, 0] * n_blocks + tile_local[:, 1]) * n_blocks + tile_local[:, 0]
    owner = key // (n_blocks * n_blocks)
    col_local = (key // n_blocks) % n_blocks
    row_local = key % n_blocks
    tile_ids = jnp.arange(n_tiles, dtype=jnp.int32)
    same = owner[:, None] == owner[None, :]
    rank = jnp.sum((same & (tile_ids[None, :] < tile_ids[:, None])).astype(jnp.int32), axis=1)
    slot = owner * capacity + rank
    slot_range = jnp.arange(n_row * capacity, dtype=jnp.int32)
    slot_hot = slot[None, :] == slot_range[:, None]
    lane_slots = jnp.broadcast_to(slot_range.reshape(n_row, capacity, 1), (n_row, capacity, 128))
    requests = jnp.sum(
        jnp.where(slot[None, None, None, :] == lane_slots[..., None], col_local[None, None, None, :], 0),
        axis=-1,
    )
    own_blocks = rows_of(xb, row_local)
    mirror_terms = jnp.einsum(
        "tfi,tij->tfj", own_blocks, tiles, preferred_element_type=jnp.float32
    ).astype(jnp.bfloat16)
    outgoing = jnp.zeros((n_row * capacity, feat_q, tile_dim), jnp.bfloat16)
    outgoing = outgoing.at[slot].set(mirror_terms, mode="promise_in_bounds", unique_indices=True)
    mirror_half = outgoing.reshape(n_row, capacity, feat_q, tile_dim)
    got_ids = lax.all_to_all(requests, "row", split_axis=0, concat_axis=0, tiled=True)
    block_ids = got_ids[:, :, 0]
    asked = rows_of(xb, block_ids.reshape(-1)).reshape(n_row, capacity, feat_q, tile_dim)
    payload = jnp.concatenate([asked, mirror_half], axis=1)
    both = lax.all_to_all(payload, "row", split_axis=0, concat_axis=0, tiled=True)
    fetched = both[:, :capacity].reshape(n_row * capacity, feat_q, tile_dim)
    incoming = both[:, capacity:].reshape(n_row * capacity, feat_q, tile_dim)
    tile_of_slot = jnp.sum(jnp.where(slot_hot, tile_ids[None, :], 0), axis=1)
    slot_used = jnp.any(slot_hot, axis=1)
    tiles_by_slot = jnp.where(slot_used[:, None, None], rows_of(tiles, tile_of_slot), 0)
    row_of_slot = jnp.where(slot_used, rows_of(row_local, tile_of_slot), -1)
    forward_terms = jnp.einsum(
        "sfj,sij->sfi", fetched, tiles_by_slot, preferred_element_type=jnp.float32
    )
    block_range = jnp.arange(n_blocks, dtype=jnp.int32)
    terms = jnp.concatenate([forward_terms, incoming.astype(jnp.float32)], axis=0)
    targets = jnp.concatenate([row_of_slot, block_ids.reshape(-1)], axis=0)
    target_hot = (targets[:, None] == block_range[None, :]).astype(jnp.float32)
    z_sum = jnp.einsum("sfi,sb->fbi", terms, target_hot, precision=lax.Precision.HIGHEST)
    z_part = z_sum.reshape(feat_q, rows).astype(jnp.bfloat16)
    z_full = gather_groups(z_part, n_col)
    y_full = lax.dot_general(
        z_full, weight, (((0,), (0,)), ((), ())), preferred_element_type=jnp.float32
    )
    act = jax.nn.silu(y_full).astype(jnp.bfloat16)
    sig = jax.nn.sigmoid(y_full)
    grad_y = (cotangent.astype(jnp.float32) * sig * (1.0 + y_full * (1.0 - sig))).astype(
        jnp.bfloat16
    )
    grad_part = jnp.dot(z_part, grad_y, preferred_element_type=jnp.float32)
    grad_w = sum_over_row(grad_part, n_row)
    return (act, grad_w)


def solution(mesh):
    in_specs = (
        P("col", "row"),
        P("row", None, None),
        P("row", None),
        P("row", None),
        P(),
        P("row", None),
    )
    out_specs = (P("row", None), P("col", None))
    return jax.shard_map(body, mesh=mesh, in_specs=in_specs, out_specs=out_specs, check_vma=False)
```

```python
import jax
import jax.numpy as jnp
from jax import lax
from jax.sharding import PartitionSpec as P


def rows_of(a, idx):
    return a.at[idx].get(mode="promise_in_bounds")


def gather_groups(z_part, n_col):
    if n_col == 1:
        return z_part
    me = lax.axis_index("col")
    if n_col & (n_col - 1):
        parts = [z_part]
        for k in range(1, n_col):
            perm = [(i, (i + k) % n_col) for i in range(n_col)]
            parts.append(lax.ppermute(z_part, "col", perm))
        order = (me - jnp.arange(n_col, dtype=jnp.int32)) % n_col
        full = rows_of(jnp.stack(parts), order)
        return full.reshape(n_col * z_part.shape[0], z_part.shape[1])
    if n_col == 4:
        across = lax.ppermute(z_part, "col", [(i, i ^ 2) for i in range(n_col)])
        beside = lax.ppermute(z_part, "col", [(i, i ^ 1) for i in range(n_col)])
        corner = lax.ppermute(across, "col", [(i, i ^ 1) for i in range(n_col)])
        parts = [z_part, beside, across, corner]
    else:
        parts = [z_part]
        for k in range(1, n_col):
            parts.append(lax.ppermute(z_part, "col", [(i, i ^ k) for i in range(n_col)]))
    groups = []
    for j in range(n_col):
        pick = parts[n_col - 1]
        for k in range(n_col - 2, -1, -1):
            pick = jnp.where((me ^ k) == j, parts[k], pick)
        groups.append(pick)
    return jnp.concatenate(groups, axis=0)


def sum_over_row(x, n_row):
    every = jnp.broadcast_to(x[None], (n_row,) + x.shape)
    parts = lax.all_to_all(every, "row", split_axis=0, concat_axis=0, tiled=True)
    total = parts[0]
    for i in range(1, n_row):
        total = total + parts[i]
    return total


def body(x_t, tiles, tile_owner, tile_local, weight, cotangent):
    n_row = lax.axis_size("row")
    n_col = lax.axis_size("col")
    n_tiles, tile_dim = (tiles.shape[0], tiles.shape[1])
    feat_q, rows = x_t.shape
    n_blocks = rows // tile_dim
    capacity = 2 * (n_tiles // n_row)
    xb = x_t.reshape(feat_q, n_blocks, tile_dim).transpose(1, 0, 2)
    flat_blocks = xb.reshape(n_blocks, feat_q * tile_dim)
    key = (tile_owner[:, 0] * n_blocks + tile_local[:, 1]) * n_blocks + tile_local[:, 0]
    owner = key // (n_blocks * n_blocks)
    col_local = (key // n_blocks) % n_blocks
    row_local = key % n_blocks
    tile_ids = jnp.arange(n_tiles, dtype=jnp.int32)
    same = owner[:, None] == owner[None, :]
    rank = jnp.sum((same & (tile_ids[None, :] < tile_ids[:, None])).astype(jnp.int32), axis=1)
    slot = owner * capacity + rank
    slot_range = jnp.arange(n_row * capacity, dtype=jnp.int32)
    slot_hot = slot[None, :] == slot_range[:, None]
    lane_slots = jnp.broadcast_to(slot_range.reshape(n_row, capacity, 1), (n_row, capacity, 128))
    requests = jnp.sum(
        jnp.where(slot[None, None, None, :] == lane_slots[..., None], col_local[None, None, None, :], 0),
        axis=-1,
    )
    own_blocks = rows_of(xb, row_local)
    mirror_terms = jnp.einsum(
        "tfi,tij->tfj", own_blocks, tiles, preferred_element_type=jnp.float32
    ).astype(jnp.bfloat16)
    outgoing = jnp.zeros((n_row * capacity, feat_q, tile_dim), jnp.bfloat16)
    outgoing = outgoing.at[slot].set(mirror_terms, mode="promise_in_bounds", unique_indices=True)
    base = jnp.concatenate(
        [jnp.zeros_like(outgoing), outgoing], axis=0
    ).reshape(2, n_row, capacity, feat_q, tile_dim).transpose(1, 0, 2, 3, 4)
    base = base.reshape(n_row, 2 * capacity, feat_q, tile_dim)
    got_ids = lax.all_to_all(requests, "row", split_axis=0, concat_axis=0, tiled=True)
    block_ids = got_ids[:, :, 0]
    asked = rows_of(xb, block_ids.reshape(-1)).reshape(n_row, capacity, feat_q, tile_dim)
    payload = lax.dynamic_update_slice(base, asked, (0, 0, 0, 0))
    both = lax.all_to_all(payload, "row", split_axis=0, concat_axis=0, tiled=True)
    fetched = both[:, :capacity].reshape(n_row * capacity, feat_q, tile_dim)
    incoming = both[:, capacity:].reshape(n_row * capacity, feat_q, tile_dim)
    tile_of_slot = jnp.sum(jnp.where(slot_hot, tile_ids[None, :], 0), axis=1)
    slot_used = jnp.any(slot_hot, axis=1)
    tiles_by_slot = jnp.where(slot_used[:, None, None], rows_of(tiles, tile_of_slot), 0)
    row_of_slot = jnp.where(slot_used, rows_of(row_local, tile_of_slot), -1)
    forward_terms = jnp.einsum(
        "sfj,sij->sfi", fetched, tiles_by_slot, preferred_element_type=jnp.float32
    )
    block_range = jnp.arange(n_blocks, dtype=jnp.int32)
    terms = jnp.concatenate([forward_terms, incoming.astype(jnp.float32)], axis=0)
    targets = jnp.concatenate([row_of_slot, block_ids.reshape(-1)], axis=0)
    target_hot = targets[:, None] == block_range[None, :]
    z_sum = jnp.sum(jnp.where(target_hot[:, None, :, None], terms[:, :, None, :], 0.0), axis=0)
    z_part = z_sum.reshape(feat_q, rows).astype(jnp.bfloat16)
    z_full = gather_groups(z_part, n_col)
    y_full = lax.dot_general(
        z_full, weight, (((0,), (0,)), ((), ())), preferred_element_type=jnp.float32
    )
    act = jax.nn.silu(y_full).astype(jnp.bfloat16)
    sig = jax.nn.sigmoid(y_full)
    grad_y = (cotangent.astype(jnp.float32) * sig * (1.0 + y_full * (1.0 - sig))).astype(
        jnp.bfloat16
    )
    grad_part = jnp.dot(z_part, grad_y, preferred_element_type=jnp.float32)
    grad_w = sum_over_row(grad_part, n_row)
    return (act, grad_w)


def solution(mesh):
    in_specs = (
        P("col", "row"),
        P("row", None, None),
        P("row", None),
        P("row", None),
        P(),
        P("row", None),
    )
    out_specs = (P("row", None), P("col", None))
    return jax.shard_map(body, mesh=mesh, in_specs=in_specs, out_specs=out_specs, check_vma=False)
```

```python
import jax
import jax.numpy as jnp
from jax import lax
from jax.sharding import PartitionSpec as P


def rows_of(a, idx):
    return a.at[idx].get(mode="promise_in_bounds")


def gather_groups(z_part, n_col):
    if n_col == 1:
        return z_part
    me = lax.axis_index("col")
    if n_col & (n_col - 1):
        parts = [z_part]
        for k in range(1, n_col):
            perm = [(i, (i + k) % n_col) for i in range(n_col)]
            parts.append(lax.ppermute(z_part, "col", perm))
        order = (me - jnp.arange(n_col, dtype=jnp.int32)) % n_col
        full = rows_of(jnp.stack(parts), order)
        return full.reshape(n_col * z_part.shape[0], z_part.shape[1])
    if n_col == 4:
        across = lax.ppermute(z_part, "col", [(i, i ^ 2) for i in range(n_col)])
        beside = lax.ppermute(z_part, "col", [(i, i ^ 1) for i in range(n_col)])
        corner = lax.ppermute(across, "col", [(i, i ^ 1) for i in range(n_col)])
        parts = [z_part, beside, across, corner]
    else:
        parts = [z_part]
        for k in range(1, n_col):
            parts.append(lax.ppermute(z_part, "col", [(i, i ^ k) for i in range(n_col)]))
    groups = []
    for j in range(n_col):
        pick = parts[n_col - 1]
        for k in range(n_col - 2, -1, -1):
            pick = jnp.where((me ^ k) == j, parts[k], pick)
        groups.append(pick)
    return jnp.concatenate(groups, axis=0)


def sum_over_row(x, n_row):
    every = jnp.broadcast_to(x[None], (n_row,) + x.shape)
    parts = lax.all_to_all(every, "row", split_axis=0, concat_axis=0, tiled=True)
    total = parts[0]
    for i in range(1, n_row):
        total = total + parts[i]
    return total


def body(x_t, tiles, tile_owner, tile_local, weight, cotangent):
    n_row = lax.axis_size("row")
    n_col = lax.axis_size("col")
    n_tiles, tile_dim = (tiles.shape[0], tiles.shape[1])
    feat_q, rows = x_t.shape
    n_blocks = rows // tile_dim
    capacity = 2 * (n_tiles // n_row)
    xb = x_t.reshape(feat_q, n_blocks, tile_dim).transpose(1, 0, 2)
    flat_blocks = xb.reshape(n_blocks, feat_q * tile_dim)
    key = (tile_owner[:, 0] * n_blocks + tile_local[:, 1]) * n_blocks + tile_local[:, 0]
    owner = key // (n_blocks * n_blocks)
    col_local = (key // n_blocks) % n_blocks
    row_local = key % n_blocks
    tile_ids = jnp.arange(n_tiles, dtype=jnp.int32)
    same = owner[:, None] == owner[None, :]
    rank = jnp.sum((same & (tile_ids[None, :] < tile_ids[:, None])).astype(jnp.int32), axis=1)
    slot = owner * capacity + rank
    slot_range = jnp.arange(n_row * capacity, dtype=jnp.int32)
    slot_hot = slot[None, :] == slot_range[:, None]
    lane_slots = jnp.broadcast_to(slot_range.reshape(n_row, capacity, 1), (n_row, capacity, 128))
    requests = jnp.sum(
        jnp.where(slot[None, None, None, :] == lane_slots[..., None], col_local[None, None, None, :], 0),
        axis=-1,
    )
    own_blocks = rows_of(xb, row_local)
    mirror_terms = jnp.einsum(
        "tfi,tij->tfj", own_blocks, tiles, preferred_element_type=jnp.float32
    ).astype(jnp.bfloat16)
    outgoing = jnp.zeros((n_row * capacity, feat_q, tile_dim), jnp.bfloat16)
    outgoing = outgoing.at[slot].set(mirror_terms, mode="promise_in_bounds", unique_indices=True)
    base = jnp.concatenate(
        [jnp.zeros_like(outgoing), outgoing], axis=0
    ).reshape(2, n_row, capacity, feat_q, tile_dim).transpose(1, 0, 2, 3, 4)
    base = base.reshape(n_row, 2 * capacity, feat_q, tile_dim)
    got_ids = lax.all_to_all(requests, "row", split_axis=0, concat_axis=0, tiled=True)
    block_ids = got_ids[:, :, 0]
    asked = rows_of(xb, block_ids.reshape(-1)).reshape(n_row, capacity, feat_q, tile_dim)
    payload = lax.dynamic_update_slice(base, asked, (0, 0, 0, 0))
    both = lax.all_to_all(payload, "row", split_axis=0, concat_axis=0, tiled=True)
    fetched = both[:, :capacity].reshape(n_row * capacity, feat_q, tile_dim)
    incoming = both[:, capacity:].reshape(n_row * capacity, feat_q, tile_dim)
    tile_of_slot = jnp.sum(jnp.where(slot_hot, tile_ids[None, :], 0), axis=1)
    slot_used = jnp.any(slot_hot, axis=1)
    tiles_by_slot = jnp.where(slot_used[:, None, None], rows_of(tiles, tile_of_slot), 0)
    row_of_slot = jnp.where(slot_used, rows_of(row_local, tile_of_slot), -1)
    block_range = jnp.arange(n_blocks, dtype=jnp.int32)
    sources = jnp.concatenate([fetched, incoming], axis=0)
    targets = jnp.concatenate([row_of_slot, block_ids.reshape(-1)], axis=0)
    keep = targets[None, :] == block_range[:, None]
    placed = jnp.where(keep[:, :, None, None], sources[None], jnp.zeros((), sources.dtype))
    identity = jnp.broadcast_to(jnp.eye(tile_dim, dtype=sources.dtype), (n_row * capacity, tile_dim, tile_dim))
    right = jnp.concatenate([tiles_by_slot.transpose(0, 2, 1), identity], axis=0)
    z_sum = jnp.einsum("bsfk,ski->fbi", placed, right, preferred_element_type=jnp.float32)
    z_part = z_sum.reshape(feat_q, rows).astype(jnp.bfloat16)
    z_full = gather_groups(z_part, n_col)
    y_full = lax.dot_general(
        z_full, weight, (((0,), (0,)), ((), ())), preferred_element_type=jnp.float32
    )
    act = jax.nn.silu(y_full).astype(jnp.bfloat16)
    sig = jax.nn.sigmoid(y_full)
    grad_y = (cotangent.astype(jnp.float32) * sig * (1.0 + y_full * (1.0 - sig))).astype(
        jnp.bfloat16
    )
    grad_part = jnp.dot(z_part, grad_y, preferred_element_type=jnp.float32)
    grad_w = sum_over_row(grad_part, n_row)
    return (act, grad_w)


def solution(mesh):
    in_specs = (
        P("col", "row"),
        P("row", None, None),
        P("row", None),
        P("row", None),
        P(),
        P("row", None),
    )
    out_specs = (P("row", None), P("col", None))
    return jax.shard_map(body, mesh=mesh, in_specs=in_specs, out_specs=out_specs, check_vma=False)
```

```python
import jax
import jax.numpy as jnp
from jax import lax
from jax.sharding import PartitionSpec as P


def rows_of(a, idx):
    return a.at[idx].get(mode="promise_in_bounds")


def gather_groups(z_part, n_col):
    if n_col == 1:
        return z_part
    me = lax.axis_index("col")
    if n_col & (n_col - 1):
        parts = [z_part]
        for k in range(1, n_col):
            perm = [(i, (i + k) % n_col) for i in range(n_col)]
            parts.append(lax.ppermute(z_part, "col", perm))
        order = (me - jnp.arange(n_col, dtype=jnp.int32)) % n_col
        full = rows_of(jnp.stack(parts), order)
        return full.reshape(n_col * z_part.shape[0], z_part.shape[1])
    if n_col == 4:
        across = lax.ppermute(z_part, "col", [(i, i ^ 2) for i in range(n_col)])
        beside = lax.ppermute(z_part, "col", [(i, i ^ 1) for i in range(n_col)])
        corner = lax.ppermute(across, "col", [(i, i ^ 1) for i in range(n_col)])
        parts = [z_part, beside, across, corner]
    else:
        parts = [z_part]
        for k in range(1, n_col):
            parts.append(lax.ppermute(z_part, "col", [(i, i ^ k) for i in range(n_col)]))
    groups = []
    for j in range(n_col):
        pick = parts[n_col - 1]
        for k in range(n_col - 2, -1, -1):
            pick = jnp.where((me ^ k) == j, parts[k], pick)
        groups.append(pick)
    return jnp.concatenate(groups, axis=0)


def sum_over_row(x, n_row):
    if n_row & (n_row - 1):
        every = jnp.broadcast_to(x[None], (n_row,) + x.shape)
        parts = lax.all_to_all(every, "row", split_axis=0, concat_axis=0, tiled=True)
        total = parts[0]
        for i in range(1, n_row):
            total = total + parts[i]
        return total
    k = 1
    while k < n_row:
        x = x + lax.ppermute(x, "row", [(i, i ^ k) for i in range(n_row)])
        k *= 2
    return x


def body(x_t, tiles, tile_owner, tile_local, weight, cotangent):
    n_row = lax.axis_size("row")
    n_col = lax.axis_size("col")
    n_tiles, tile_dim = (tiles.shape[0], tiles.shape[1])
    feat_q, rows = x_t.shape
    n_blocks = rows // tile_dim
    capacity = 2 * (n_tiles // n_row)
    xb = x_t.reshape(feat_q, n_blocks, tile_dim).transpose(1, 0, 2)
    flat_blocks = xb.reshape(n_blocks, feat_q * tile_dim)
    key = (tile_owner[:, 0] * n_blocks + tile_local[:, 1]) * n_blocks + tile_local[:, 0]
    owner = key // (n_blocks * n_blocks)
    col_local = (key // n_blocks) % n_blocks
    row_local = key % n_blocks
    tile_ids = jnp.arange(n_tiles, dtype=jnp.int32)
    same = owner[:, None] == owner[None, :]
    rank = jnp.sum((same & (tile_ids[None, :] < tile_ids[:, None])).astype(jnp.int32), axis=1)
    slot = owner * capacity + rank
    slot_range = jnp.arange(n_row * capacity, dtype=jnp.int32)
    slot_hot = slot[None, :] == slot_range[:, None]
    lane_slots = jnp.broadcast_to(slot_range.reshape(n_row, capacity, 1), (n_row, capacity, 128))
    requests = jnp.sum(
        jnp.where(slot[None, None, None, :] == lane_slots[..., None], col_local[None, None, None, :], 0),
        axis=-1,
    )
    own_blocks = rows_of(xb, row_local)
    mirror_terms = jnp.einsum(
        "tfi,tij->tfj", own_blocks, tiles, preferred_element_type=jnp.float32
    ).astype(jnp.bfloat16)
    outgoing = jnp.zeros((n_row * capacity, feat_q, tile_dim), jnp.bfloat16)
    outgoing = outgoing.at[slot].set(mirror_terms, mode="promise_in_bounds", unique_indices=True)
    base = jnp.concatenate(
        [jnp.zeros_like(outgoing), outgoing], axis=0
    ).reshape(2, n_row, capacity, feat_q, tile_dim).transpose(1, 0, 2, 3, 4)
    base = base.reshape(n_row, 2 * capacity, feat_q, tile_dim)
    got_ids = lax.all_to_all(requests, "row", split_axis=0, concat_axis=0, tiled=True)
    block_ids = got_ids[:, :, 0]
    asked = rows_of(xb, block_ids.reshape(-1)).reshape(n_row, capacity, feat_q, tile_dim)
    payload = lax.dynamic_update_slice(base, asked, (0, 0, 0, 0))
    both = lax.all_to_all(payload, "row", split_axis=0, concat_axis=0, tiled=True)
    fetched = both[:, :capacity].reshape(n_row * capacity, feat_q, tile_dim)
    incoming = both[:, capacity:].reshape(n_row * capacity, feat_q, tile_dim)
    tile_of_slot = jnp.sum(jnp.where(slot_hot, tile_ids[None, :], 0), axis=1)
    slot_used = jnp.any(slot_hot, axis=1)
    tiles_by_slot = jnp.where(slot_used[:, None, None], rows_of(tiles, tile_of_slot), 0)
    row_of_slot = jnp.where(slot_used, rows_of(row_local, tile_of_slot), -1)
    forward_terms = jnp.einsum(
        "sfj,sij->sfi", fetched, tiles_by_slot, preferred_element_type=jnp.float32
    )
    block_range = jnp.arange(n_blocks, dtype=jnp.int32)
    terms = jnp.concatenate([forward_terms, incoming.astype(jnp.float32)], axis=0)
    targets = jnp.concatenate([row_of_slot, block_ids.reshape(-1)], axis=0)
    target_hot = (targets[:, None] == block_range[None, :]).astype(jnp.float32)
    z_sum = jnp.einsum("sfi,sb->fbi", terms, target_hot, precision=lax.Precision.HIGHEST)
    z_part = z_sum.reshape(feat_q, rows).astype(jnp.bfloat16)
    z_full = gather_groups(z_part, n_col)
    y_full = lax.dot_general(
        z_full, weight, (((0,), (0,)), ((), ())), preferred_element_type=jnp.float32
    )
    act = jax.nn.silu(y_full).astype(jnp.bfloat16)
    sig = jax.nn.sigmoid(y_full)
    grad_y = (cotangent.astype(jnp.float32) * sig * (1.0 + y_full * (1.0 - sig))).astype(
        jnp.bfloat16
    )
    grad_part = jnp.dot(z_part, grad_y, preferred_element_type=jnp.float32)
    grad_w = sum_over_row(grad_part, n_row)
    return (act, grad_w)


def solution(mesh):
    in_specs = (
        P("col", "row"),
        P("row", None, None),
        P("row", None),
        P("row", None),
        P(),
        P("row", None),
    )
    out_specs = (P("row", None), P("col", None))
    return jax.shard_map(body, mesh=mesh, in_specs=in_specs, out_specs=out_specs, check_vma=False)
```
